256 devices in a mesh: expert: 16 (over z, core), tensor: 16 (over y, x).
Axes of the slice: x: 4, y: 4, z: 8, core: 2. Of those that a mesh axis runs over, the one named last changes fastest.
Arguments:
- residual_in: bfloat16 [22528, 1024], P(('expert', 'tensor')), may hold values from -6 to 6
- attn_heads: bfloat16 [1024, 22528], P('tensor', 'expert'), may hold values from -6 to 6
- out_proj: bfloat16 [1024, 1024], P('tensor'), may hold values from -0.1875 to 0.1875
- gain_first: float32 [1024], replicated, may hold values from 0.25 to 1.75
- router_weight: float32 [1024, 16], replicated, may hold values from -0.046875 to 0.046875
- routes: int32 [22528, 2], P(('expert', 'tensor')), may hold values from 0 to 15, all different within a row; in each aligned block of 88 rows (0 to 87, 88 to 175, ...) at most 22 rows name the same one
- w_gate: bfloat16 [16, 2816, 1024], P('expert', 'tensor'), may hold values from -0.1875 to 0.1875
- w_upward: bfloat16 [16, 2816, 1024], P('expert', 'tensor'), may hold values from -0.1875 to 0.1875
- w_downward: bfloat16 [16, 2816, 1024], P('expert', 'tensor'), may hold values from -0.21875 to 0.21875
- gain_second: float32 [1024], replicated, may hold values from 0.25 to 1.75
Outputs:
- residual_out: bfloat16 [22528, 1024], P(('expert', 'tensor'))
- next_normed: bfloat16 [22528, 1024], P(('expert', 'tensor'))
The draws below stay inside these ranges and needn't reach their ends.
Inputs may be any that keep to these rules, and one draw needn't show every extreme that they name: `routes`: each row names two different experts; among the rows of one device no expert is named more than 22 times, and some expert reaches 22.
All inputs are finite; a program needn't handle non-finite values.
Results may differ from the reference program's by a relative error of at most 0.012.
Values may be sent and summed in bfloat16 or wider, within the bound.
No kernel may reach another device: no remote copies, remote signals or barrier semaphores. Data moves between devices by JAX's collectives and lax.ppermute only.
A program may use at most 128 MiB of HBM per device.

```python
import math
import jax
import jax.numpy as jnp
import numpy as np
from jax import lax

D = 1024
HEADS = 16
HEAD_DIM = 64
FF = 2816
ROWS = 88
EXPERTS = 16
CAP = 22
TOKENS = 22528


def levels(stream_key, extent, shards, least, largest):
    level = 1.0
    for axis_at, shards_of in shards:
        steps = jax.random.uniform(jax.random.fold_in(jax.random.fold_in(stream_key, 6), axis_at), (shards_of,), jnp.float32, least / len(shards), largest / len(shards))
        level = level * jnp.repeat(jnp.exp(steps), extent[axis_at] // shards_of).reshape((-1,) + (1,) * (len(extent) - 1 - axis_at))
    return level


def deal_out(own_key, own, number, rows, number_of, top, most, slope):
    ranking = jax.random.permutation(own_key, number_of)
    heavy_load, common = load_shares(number_of, rows * top, most, slope, True), load_shares(number_of, rows * top, most, slope, False)
    places = jnp.arange(number_of)

    def named(sizes, offset_by):
        used = int((sizes > 0).sum())
        fixed = max(1, used // 4)
        passed = fixed + (places - fixed + offset_by * (used - fixed)) % max(1, number_of - fixed)
        return jnp.zeros((number_of,), jnp.int32).at[ranking[jnp.where(places < fixed, places, passed)]].set(jnp.asarray(sizes, jnp.int32))

    sizes = jnp.where(number % 4 == 0, named(heavy_load, number // 4), named(common, number - number // 4 - 1))
    mixed = jax.random.permutation(jax.random.fold_in(own, 3), number_of)
    giver, receiver = mixed[0:number_of // 2 * 2:2], mixed[1:number_of // 2 * 2:2]
    room = jnp.minimum(sizes[giver] - 1, most - sizes[receiver]) // 2
    room = jnp.where((giver == ranking[0]) | (receiver == ranking[0]) | (sizes[receiver] == 0), 0, jnp.maximum(room, 0))
    passed = jax.random.randint(jax.random.fold_in(own, 4), (number_of // 2,), 0, 1 << 20) % (room + 1)
    sizes = sizes.at[giver].add(-passed).at[receiver].add(passed)
    members = jnp.searchsorted(jnp.cumsum(sizes), jnp.arange(rows * top), side="right").astype(jnp.int32)
    grid = members.reshape(top, rows).T
    grid = grid[jax.random.permutation(jax.random.fold_in(own, 1), rows)]
    offset_by = jax.random.randint(jax.random.fold_in(own, 2), (rows, 1), 0, top)
    return jnp.take_along_axis(grid, (jnp.arange(top)[None, :] + offset_by) % top, axis=1)


def load_shares(amount, total, bound, skew, full):
    portions = [(1 << 20) // math.isqrt(standing ** skew) + 1 for standing in range(1, amount + 1)]
    largest = bound if full else min(bound, max(-(-total // amount), total * portions[0] // sum(portions)))
    least = 1 if total - largest >= amount - 1 else 0
    counts, rest = [largest] + [least] * (amount - 1), total - largest - least * (amount - 1)
    while rest > 0:
        movable = [i for i in range(1, amount) if counts[i] < largest] or [i for i in range(1, amount) if counts[i] < bound]
        mass, remaining = sum([portions[i] for i in movable]), rest
        for i in movable:
            extra = min(bound - counts[i], max(1, remaining * portions[i] // mass), rest)
            counts[i] = counts[i] + extra
            rest = rest - extra
    return np.array(counts)


def gaussian(stream_key, dims, deviation, bound, pieces=(), held_as=jnp.bfloat16):
    level = levels(stream_key, dims, pieces, -0.22, 0.18) if pieces else 1.0
    result = jax.random.normal(stream_key, dims, jnp.float32) * deviation * level
    return jnp.minimum(jnp.maximum(result, -bound), bound).astype(held_as)


def setup_inputs(seed: int = 0) -> dict:
    splits = jax.random.split(jax.random.key(seed), 11)
    residual_in = gaussian(splits[0], (TOKENS, D), 1.0, 6.0, ((0, 256),))
    attn_heads = gaussian(splits[1], (HEADS * HEAD_DIM, TOKENS), 1.0, 6.0, ((0, 16), (1, 16)))
    out_proj = gaussian(splits[2], (HEADS * HEAD_DIM, D), (HEADS * HEAD_DIM) ** -0.5, 0.1875, ((0, 16),))
    gain_first = jnp.clip(1.0 + 0.15 * jax.random.normal(splits[3], (D,), jnp.float32), 0.25, 1.75)
    router_weight = gaussian(splits[4], (D, EXPERTS), (16 * D) ** -0.5, 0.046875, (), jnp.float32)
    routes_keys = jax.random.split(jax.random.fold_in(splits[5], 1), TOKENS // ROWS)
    routes_turns = jax.random.permutation(jax.random.fold_in(splits[5], 3), TOKENS // ROWS)
    routes = jax.vmap(lambda own, number: deal_out(jax.random.fold_in(splits[5], 2), own, number, ROWS, EXPERTS, 2, CAP, 2))(routes_keys, routes_turns).reshape((TOKENS, 2))
    w_gate = gaussian(splits[6], (EXPERTS, FF, D), D ** -0.5, 0.1875, ((0, 16), (1, 16)))
    w_upward = gaussian(splits[7], (EXPERTS, FF, D), D ** -0.5, 0.1875, ((0, 16), (1, 16)))
    w_downward = gaussian(splits[8], (EXPERTS, FF, D), (FF // 4) ** -0.5, 0.21875, ((0, 16), (1, 16)))
    gain_second = jnp.clip(1.0 + 0.15 * jax.random.normal(splits[9], (D,), jnp.float32), 0.25, 1.75)
    return {"residual_in": residual_in, "attn_heads": attn_heads, "out_proj": out_proj, "gain_first": gain_first, "router_weight": router_weight, "routes": routes, "w_gate": w_gate, "w_upward": w_upward, "w_downward": w_downward, "gain_second": gain_second}


def rms_scale(values, gain):
    wide = values.astype(jnp.float32)
    scale = lax.rsqrt(lax.optimization_barrier(jnp.mean(wide * wide, axis=-1, keepdims=True)) + 1e-06)
    return (wide * scale * gain).astype(jnp.bfloat16)

def reference(residual_in, attn_heads, out_proj, gain_first, router_weight, routes, w_gate, w_upward, w_downward, gain_second):
    projected = lax.dot_general(attn_heads, out_proj, (((0,), (0,)), ((), ())), preferred_element_type=jnp.float32)
    hidden_one = (residual_in.astype(jnp.float32) + projected).astype(jnp.bfloat16)
    normed = rms_scale(hidden_one, gain_first)
    logits = jnp.dot(normed.astype(jnp.float32), router_weight, precision=lax.Precision.HIGHEST)
    router_probs = jax.nn.softmax(logits, axis=-1)
    picked = jnp.take_along_axis(router_probs, routes, axis=1)
    gate_weights = picked / lax.optimization_barrier(jnp.sum(picked, axis=1, keepdims=True))
    flat_ids = routes.reshape(-1)
    total = flat_ids.shape[0]
    most_rows = TOKENS // ROWS * CAP

    def one_expert(carry, expert_id):
        chosen = jnp.nonzero(flat_ids == expert_id, size=most_rows, fill_value=total)[0].astype(jnp.int32)
        row_index = jnp.minimum(chosen // 2, TOKENS - 1).astype(jnp.int32)
        inputs = normed[row_index]
        w_one = w_gate[expert_id]
        u_one = w_upward[expert_id]
        d_one = w_downward[expert_id]
        gate_part = lax.dot_general(inputs, w_one, (((1,), (1,)), ((), ())), preferred_element_type=jnp.float32)
        up_part = lax.dot_general(inputs, u_one, (((1,), (1,)), ((), ())), preferred_element_type=jnp.float32)
        hid = (jax.nn.gelu(gate_part, approximate=True) * up_part).astype(jnp.bfloat16)
        outputs = jnp.dot(hid, d_one, preferred_element_type=jnp.float32).astype(jnp.bfloat16)
        carry = carry.at[chosen].set(outputs, mode='drop')
        return (carry, None)
    start = jnp.zeros((total, D), jnp.bfloat16)
    expert_out, _ = lax.scan(one_expert, start, jnp.arange(EXPERTS, dtype=jnp.int32))
    expert_out = expert_out.reshape(TOKENS, 2, D).astype(jnp.float32)
    mixed = lax.optimization_barrier(jnp.sum(gate_weights[:, :, None] * expert_out, axis=1))
    residual_out = (hidden_one.astype(jnp.float32) + mixed).astype(jnp.bfloat16)
    next_normed = rms_scale(residual_out, gain_second)
    return (residual_out, next_normed)
```

```python
import math

import jax
import jax.numpy as jnp
from jax import lax
from jax.sharding import Mesh
from jax.sharding import PartitionSpec as P

ROWS_AXES = ("expert", "ty", "tx")
TENSOR_AXES = ("ty", "tx")


def rms_scale(values, gain):
    wide = values.astype(jnp.float32)
    scale = lax.rsqrt(jnp.mean(wide * wide, axis=-1, keepdims=True) + 1e-06)
    return (wide * scale * gain).astype(jnp.bfloat16)


def expert_block(inputs, gate_rows, up_rows, down_rows):
    gate_part = lax.dot_general(
        inputs, gate_rows, (((1,), (1,)), ((), ())), preferred_element_type=jnp.float32
    )
    up_part = lax.dot_general(
        inputs, up_rows, (((1,), (1,)), ((), ())), preferred_element_type=jnp.float32
    )
    hid = (jax.nn.gelu(gate_part, approximate=True) * up_part).astype(jnp.bfloat16)
    return jnp.dot(hid, down_rows, preferred_element_type=jnp.float32)


def per_device(
    residual_in,
    attn_heads,
    out_proj,
    gain_first,
    router_weight,
    routes,
    w_gate,
    w_upward,
    w_downward,
    gain_second,
):
    row_count = residual_in.shape[0]
    width = residual_in.shape[1]
    n_expert = lax.axis_size("expert")
    capacity = 4 * row_count // n_expert

    full_proj = lax.all_gather(out_proj, TENSOR_AXES, axis=0, tiled=True)
    own_heads = lax.all_to_all(attn_heads, TENSOR_AXES, 1, 0, tiled=True)
    projected = lax.dot_general(
        own_heads, full_proj, (((0,), (0,)), ((), ())), preferred_element_type=jnp.float32
    )

    stacked = jnp.concatenate([w_gate, w_upward, w_downward], axis=0)
    weights = lax.all_gather(stacked, "tx", axis=1, tiled=True)
    gate_rows, up_rows, down_rows = weights[0], weights[1], weights[2]

    hidden_one = (residual_in.astype(jnp.float32) + projected).astype(jnp.bfloat16)
    normed = rms_scale(hidden_one, gain_first)
    logits = jnp.dot(normed.astype(jnp.float32), router_weight, precision=lax.Precision.HIGHEST)
    router_probs = jax.nn.softmax(logits, axis=-1)
    picked = jnp.take_along_axis(router_probs, routes, axis=1)
    gate_weights = picked / jnp.sum(picked, axis=1, keepdims=True)
    flat_ids = routes.reshape(-1)
    expert_iota = jnp.arange(n_expert, dtype=jnp.int32)
    onehot = (flat_ids[:, None] == expert_iota[None, :]).astype(jnp.int32)
    earlier = jnp.cumsum(onehot, axis=0) - onehot
    slot_index = jnp.sum(earlier * onehot, axis=1)
    target = flat_ids * capacity + slot_index
    slot_iota = jnp.arange(n_expert * capacity, dtype=jnp.int32)
    placing = (slot_iota[:, None] == target[None, :]).astype(jnp.bfloat16)
    repeated = jnp.repeat(normed, 2, axis=0)
    send_slots = jnp.dot(placing, repeated, preferred_element_type=jnp.float32).astype(jnp.bfloat16)
    send_slots = send_slots.reshape(n_expert, capacity, width)
    received = lax.all_to_all(send_slots, "expert", split_axis=0, concat_axis=0, tiled=True)
    slot_total = n_expert * capacity
    rows_in = received.reshape(slot_total, width)
    all_rows = lax.all_gather(rows_in, "ty", axis=0, tiled=True)
    expert_sum = lax.psum_scatter(
        expert_block(all_rows, gate_rows, up_rows, down_rows).astype(jnp.bfloat16),
        "ty",
        scatter_dimension=0,
        tiled=True,
    )
    expert_out = expert_sum.reshape(n_expert, capacity, width)
    returned = lax.all_to_all(expert_out, "expert", split_axis=0, concat_axis=0, tiled=True)
    returned = returned.reshape(slot_total, width)
    per_route = lax.dot_general(
        placing, returned, (((0,), (0,)), ((), ())), preferred_element_type=jnp.float32
    )
    per_route = per_route.reshape(row_count, 2, width)
    mixed = jnp.sum(gate_weights[:, :, None] * per_route, axis=1)
    residual_out = (hidden_one.astype(jnp.float32) + mixed).astype(jnp.bfloat16)
    next_normed = rms_scale(residual_out, gain_second)
    return (residual_out, next_normed)


def split_tensor(n):
    inner = int(math.isqrt(n))
    while n % inner:
        inner -= 1
    return n // inner, inner


def solution(mesh):
    n_expert = mesh.shape["expert"]
    n_ty, n_tx = split_tensor(mesh.shape["tensor"])
    grid = Mesh(mesh.devices.reshape(n_expert, n_ty, n_tx), ROWS_AXES)
    rows = P(ROWS_AXES, None)
    placed = (
        rows,
        P(TENSOR_AXES, "expert"),
        P(TENSOR_AXES, None),
        P(),
        P(),
        rows,
        P("expert", TENSOR_AXES, None),
        P("expert", TENSOR_AXES, None),
        P("expert", TENSOR_AXES, None),
        P(),
    )
    return jax.shard_map(
        per_device,
        mesh=grid,
        in_specs=placed,
        out_specs=(rows, rows),
        check_vma=False,
    )
```

```python
import math

import jax
import jax.numpy as jnp
from jax import lax
from jax.sharding import Mesh
from jax.sharding import PartitionSpec as P

ROWS_AXES = ("expert", "ty", "tx")
TENSOR_AXES = ("ty", "tx")


def rms_scale(values, gain):
    wide = values.astype(jnp.float32)
    scale = lax.rsqrt(jnp.mean(wide * wide, axis=-1, keepdims=True) + 1e-06)
    return (wide * scale * gain).astype(jnp.bfloat16)


def expert_block(inputs, gate_rows, up_rows, down_rows):
    gate_part = lax.dot_general(
        inputs, gate_rows, (((1,), (1,)), ((), ())), preferred_element_type=jnp.float32
    )
    up_part = lax.dot_general(
        inputs, up_rows, (((1,), (1,)), ((), ())), preferred_element_type=jnp.float32
    )
    hid = (jax.nn.gelu(gate_part, approximate=True) * up_part).astype(jnp.bfloat16)
    return jnp.dot(hid, down_rows, preferred_element_type=jnp.float32)


def per_device(
    residual_in,
    attn_heads,
    out_proj,
    gain_first,
    router_weight,
    routes,
    w_gate,
    w_upward,
    w_downward,
    gain_second,
):
    row_count = residual_in.shape[0]
    width = residual_in.shape[1]
    n_expert = lax.axis_size("expert")
    capacity = 4 * row_count // n_expert

    core = lax.axis_index("expert") % 2
    half = width // 2
    my_cols = lax.dynamic_slice_in_dim(out_proj, core * half, half, axis=1)
    my_half = lax.all_gather(my_cols, TENSOR_AXES, axis=0, tiled=True)
    other_half = lax.ppermute(my_half, "expert", [(i, i ^ 1) for i in range(n_expert)])
    own_heads = lax.all_to_all(attn_heads, TENSOR_AXES, 1, 0, tiled=True)
    contract = (((0,), (0,)), ((), ()))
    proj_mine = lax.dot_general(own_heads, my_half, contract, preferred_element_type=jnp.float32)
    proj_other = lax.dot_general(own_heads, other_half, contract, preferred_element_type=jnp.float32)
    projected = jnp.where(
        core == 0,
        jnp.concatenate([proj_mine, proj_other], axis=1),
        jnp.concatenate([proj_other, proj_mine], axis=1),
    )

    stacked = jnp.concatenate([w_gate, w_upward, w_downward], axis=0)
    n_tx = lax.axis_size("tx")
    pieces = [stacked]
    for shift in range(1, n_tx):
        pieces.append(lax.ppermute(stacked, "tx", [(i, (i + shift) % n_tx) for i in range(n_tx)]))

    hidden_one = (residual_in.astype(jnp.float32) + projected).astype(jnp.bfloat16)
    normed = rms_scale(hidden_one, gain_first)
    logits = jnp.dot(normed.astype(jnp.float32), router_weight, precision=lax.Precision.HIGHEST)
    router_probs = jax.nn.softmax(logits, axis=-1)
    picked = jnp.take_along_axis(router_probs, routes, axis=1)
    gate_weights = picked / jnp.sum(picked, axis=1, keepdims=True)
    flat_ids = routes.reshape(-1)
    expert_iota = jnp.arange(n_expert, dtype=jnp.int32)
    onehot = (flat_ids[:, None] == expert_iota[None, :]).astype(jnp.int32)
    earlier = jnp.cumsum(onehot, axis=0) - onehot
    slot_index = jnp.sum(earlier * onehot, axis=1)
    target = flat_ids * capacity + slot_index
    slot_iota = jnp.arange(n_expert * capacity, dtype=jnp.int32)
    placing = (slot_iota[:, None] == target[None, :]).astype(jnp.bfloat16)
    repeated = jnp.repeat(normed, 2, axis=0)
    send_slots = jnp.dot(placing, repeated, preferred_element_type=jnp.float32).astype(jnp.bfloat16)
    send_slots = send_slots.reshape(n_expert, capacity, width)
    send_slots, *pieces = lax.optimization_barrier((send_slots, *pieces))
    weights = jnp.concatenate(pieces, axis=1)
    gate_rows, up_rows, down_rows = weights[0], weights[1], weights[2]
    received = lax.all_to_all(send_slots, "expert", split_axis=0, concat_axis=0, tiled=True)
    slot_total = n_expert * capacity
    rows_in = received.reshape(slot_total, width)
    all_rows = lax.all_gather(rows_in, "ty", axis=0, tiled=True)
    expert_sum = lax.psum_scatter(
        expert_block(all_rows, gate_rows, up_rows, down_rows).astype(jnp.bfloat16),
        "ty",
        scatter_dimension=0,
        tiled=True,
    )
    expert_out = expert_sum.reshape(n_expert, capacity, width)
    returned = lax.all_to_all(expert_out, "expert", split_axis=0, concat_axis=0, tiled=True)
    returned = returned.reshape(slot_total, width)
    per_route = lax.dot_general(
        placing, returned, (((0,), (0,)), ((), ())), preferred_element_type=jnp.float32
    )
    per_route = per_route.reshape(row_count, 2, width)
    mixed = jnp.sum(gate_weights[:, :, None] * per_route, axis=1)
    residual_out = (hidden_one.astype(jnp.float32) + mixed).astype(jnp.bfloat16)
    next_normed = rms_scale(residual_out, gain_second)
    return (residual_out, next_normed)


def split_tensor(n):
    inner = int(math.isqrt(n))
    while n % inner:
        inner -= 1
    return n // inner, inner


def solution(mesh):
    n_expert = mesh.shape["expert"]
    n_ty, n_tx = split_tensor(mesh.shape["tensor"])
    grid = Mesh(mesh.devices.reshape(n_expert, n_ty, n_tx), ROWS_AXES)
    rows = P(ROWS_AXES, None)
    placed = (
        rows,
        P(TENSOR_AXES, "expert"),
        P(TENSOR_AXES, None),
        P(),
        P(),
        rows,
        P("expert", TENSOR_AXES, None),
        P("expert", TENSOR_AXES, None),
        P("expert", TENSOR_AXES, None),
        P(),
    )
    return jax.shard_map(
        per_device,
        mesh=grid,
        in_specs=placed,
        out_specs=(rows, rows),
        check_vma=False,
    )
```

```python
import math

import jax
import jax.numpy as jnp
from jax import lax
from jax.sharding import Mesh
from jax.sharding import PartitionSpec as P

ROWS_AXES = ("expert", "ty", "tx")
TENSOR_AXES = ("ty", "tx")


def rms_scale(values, gain):
    wide = values.astype(jnp.float32)
    scale = lax.rsqrt(jnp.mean(wide * wide, axis=-1, keepdims=True) + 1e-06)
    return (wide * scale * gain).astype(jnp.bfloat16)


def expert_block(inputs, gate_rows, up_rows, down_rows):
    gate_part = lax.dot_general(
        inputs, gate_rows, (((1,), (1,)), ((), ())), preferred_element_type=jnp.float32
    )
    up_part = lax.dot_general(
        inputs, up_rows, (((1,), (1,)), ((), ())), preferred_element_type=jnp.float32
    )
    hid = (jax.nn.gelu(gate_part, approximate=True) * up_part).astype(jnp.bfloat16)
    return jnp.dot(hid, down_rows, preferred_element_type=jnp.float32)


def per_device(
    residual_in,
    attn_heads,
    out_proj,
    gain_first,
    router_weight,
    routes,
    w_gate,
    w_upward,
    w_downward,
    gain_second,
):
    row_count = residual_in.shape[0]
    width = residual_in.shape[1]
    n_expert = lax.axis_size("expert")
    capacity = 4 * row_count // n_expert

    n_ty = lax.axis_size("ty")
    n_tx = lax.axis_size("tx")
    ty = lax.axis_index("ty")
    tx = lax.axis_index("tx")
    near = [out_proj] + [
        lax.ppermute(out_proj, "tx", shift_pairs(n_tx, s)) for s in range(1, n_tx)
    ]
    near = jnp.stack(near)
    full_proj = [near] + [lax.ppermute(near, "ty", shift_pairs(n_ty, s)) for s in range(1, n_ty)]
    full_proj = jnp.stack(full_proj)
    own_heads = lax.all_to_all(attn_heads, TENSOR_AXES, 1, 0, tiled=True)
    own_heads = own_heads.reshape(n_ty, n_tx, -1, row_count)
    from_y = (ty - jnp.arange(n_ty)) % n_ty
    from_x = (tx - jnp.arange(n_tx)) % n_tx
    own_heads = jnp.take(jnp.take(own_heads, from_y, axis=0), from_x, axis=1)
    projected = lax.dot_general(
        own_heads, full_proj, (((0, 1, 2), (0, 1, 2)), ((), ())), preferred_element_type=jnp.float32
    )

    stacked = jnp.concatenate([w_gate, w_upward, w_downward], axis=0)
    pieces = [stacked] + [
        lax.ppermute(stacked, "tx", shift_pairs(n_tx, s)) for s in range(1, n_tx)
    ]

    hidden_one = (residual_in.astype(jnp.float32) + projected).astype(jnp.bfloat16)
    normed = rms_scale(hidden_one, gain_first)
    logits = jnp.dot(normed.astype(jnp.float32), router_weight, precision=lax.Precision.HIGHEST)
    router_probs = jax.nn.softmax(logits, axis=-1)
    picked = jnp.take_along_axis(router_probs, routes, axis=1)
    gate_weights = picked / jnp.sum(picked, axis=1, keepdims=True)
    flat_ids = routes.reshape(-1)
    expert_iota = jnp.arange(n_expert, dtype=jnp.int32)
    onehot = (flat_ids[:, None] == expert_iota[None, :]).astype(jnp.int32)
    earlier = jnp.cumsum(onehot, axis=0) - onehot
    slot_index = jnp.sum(earlier * onehot, axis=1)
    target = flat_ids * capacity + slot_index
    slot_iota = jnp.arange(n_expert * capacity, dtype=jnp.int32)
    placing = (slot_iota[:, None] == target[None, :]).astype(jnp.bfloat16)
    repeated = jnp.repeat(normed, 2, axis=0)
    send_slots = jnp.dot(placing, repeated, preferred_element_type=jnp.float32).astype(jnp.bfloat16)
    send_slots = send_slots.reshape(n_expert, capacity, width)
    weights = jnp.concatenate(pieces, axis=1)
    gate_rows, up_rows, down_rows = weights[0], weights[1], weights[2]
    received = lax.all_to_all(send_slots, "expert", split_axis=0, concat_axis=0, tiled=True)
    slot_total = n_expert * capacity
    rows_in = received.reshape(slot_total, width)
    all_rows = [rows_in] + [lax.ppermute(rows_in, "ty", shift_pairs(n_ty, s)) for s in range(1, n_ty)]
    all_rows = jnp.concatenate(all_rows, axis=0)
    partial = expert_block(all_rows, gate_rows, up_rows, down_rows).astype(jnp.bfloat16)
    partial = partial.reshape(n_ty, slot_total, width)
    expert_sum = partial[0].astype(jnp.float32)
    for s in range(1, n_ty):
        back = lax.ppermute(partial[s], "ty", shift_pairs(n_ty, -s))
        expert_sum = expert_sum + back.astype(jnp.float32)
    expert_sum = expert_sum.astype(jnp.bfloat16)
    expert_out = expert_sum.reshape(n_expert, capacity, width)
    returned = lax.all_to_all(expert_out, "expert", split_axis=0, concat_axis=0, tiled=True)
    returned = returned.reshape(slot_total, width)
    per_route = lax.dot_general(
        placing, returned, (((0,), (0,)), ((), ())), preferred_element_type=jnp.float32
    )
    per_route = per_route.reshape(row_count, 2, width)
    mixed = jnp.sum(gate_weights[:, :, None] * per_route, axis=1)
    residual_out = (hidden_one.astype(jnp.float32) + mixed).astype(jnp.bfloat16)
    next_normed = rms_scale(residual_out, gain_second)
    return (residual_out, next_normed)


def shift_pairs(n, shift):
    return [(i, (i + shift) % n) for i in range(n)]


def split_tensor(n):
    inner = int(math.isqrt(n))
    while n % inner:
        inner -= 1
    return n // inner, inner


def solution(mesh):
    n_expert = mesh.shape["expert"]
    n_ty, n_tx = split_tensor(mesh.shape["tensor"])
    grid = Mesh(mesh.devices.reshape(n_expert, n_ty, n_tx), ROWS_AXES)
    rows = P(ROWS_AXES, None)
    placed = (
        rows,
        P(TENSOR_AXES, "expert"),
        P(TENSOR_AXES, None),
        P(),
        P(),
        rows,
        P("expert", TENSOR_AXES, None),
        P("expert", TENSOR_AXES, None),
        P("expert", TENSOR_AXES, None),
        P(),
    )
    return jax.shard_map(
        per_device,
        mesh=grid,
        in_specs=placed,
        out_specs=(rows, rows),
        check_vma=False,
    )
```

```python
import math

import jax
import jax.numpy as jnp
from jax import lax
from jax.sharding import Mesh
from jax.sharding import PartitionSpec as P

ROWS_AXES = ("expert", "ty", "tx")
TENSOR_AXES = ("ty", "tx")


def rms_scale(values, gain):
    wide = values.astype(jnp.float32)
    scale = lax.rsqrt(jnp.mean(wide * wide, axis=-1, keepdims=True) + 1e-06)
    return (wide * scale * gain).astype(jnp.bfloat16)


def expert_block(inputs, gate_rows, up_rows, down_rows):
    gate_part = lax.dot_general(
        inputs, gate_rows, (((1,), (1,)), ((), ())), preferred_element_type=jnp.float32
    )
    up_part = lax.dot_general(
        inputs, up_rows, (((1,), (1,)), ((), ())), preferred_element_type=jnp.float32
    )
    hid = (jax.nn.gelu(gate_part, approximate=True) * up_part).astype(jnp.bfloat16)
    return jnp.dot(hid, down_rows, preferred_element_type=jnp.float32)


def per_device(
    residual_in,
    attn_heads,
    out_proj,
    gain_first,
    router_weight,
    routes,
    w_gate,
    w_upward,
    w_downward,
    gain_second,
):
    row_count = residual_in.shape[0]
    width = residual_in.shape[1]
    n_expert = lax.axis_size("expert")
    capacity = 4 * row_count // n_expert

    n_ty = lax.axis_size("ty")
    n_tx = lax.axis_size("tx")
    ty = lax.axis_index("ty")
    tx = lax.axis_index("tx")
    core = lax.axis_index("expert") % 2
    half = width // 2
    my_cols = lax.dynamic_slice_in_dim(out_proj, core * half, half, axis=1)
    near = [my_cols] + [lax.ppermute(my_cols, "tx", shift_pairs(n_tx, s)) for s in range(1, n_tx)]
    near = jnp.stack(near)
    my_half = [near] + [lax.ppermute(near, "ty", shift_pairs(n_ty, s)) for s in range(1, n_ty)]
    my_half = jnp.stack(my_half)
    other_half = lax.ppermute(my_half, "expert", [(i, i ^ 1) for i in range(n_expert)])
    own_heads = lax.all_to_all(attn_heads, TENSOR_AXES, 1, 0, tiled=True)
    own_heads = own_heads.reshape(n_ty, n_tx, -1, row_count)
    from_y = (ty - jnp.arange(n_ty)) % n_ty
    from_x = (tx - jnp.arange(n_tx)) % n_tx
    own_heads = jnp.take(jnp.take(own_heads, from_y, axis=0), from_x, axis=1)
    contract = (((0, 1, 2), (0, 1, 2)), ((), ()))
    proj_mine = lax.dot_general(own_heads, my_half, contract, preferred_element_type=jnp.float32)
    proj_other = lax.dot_general(own_heads, other_half, contract, preferred_element_type=jnp.float32)
    projected = jnp.where(
        core == 0,
        jnp.concatenate([proj_mine, proj_other], axis=1),
        jnp.concatenate([proj_other, proj_mine], axis=1),
    )

    stacked = jnp.concatenate([w_gate, w_upward, w_downward], axis=0)
    stacked, near = lax.optimization_barrier((stacked, near))
    pieces = [stacked] + [
        lax.ppermute(stacked, "tx", shift_pairs(n_tx, s)) for s in range(1, n_tx)
    ]

    hidden_one = (residual_in.astype(jnp.float32) + projected).astype(jnp.bfloat16)
    normed = rms_scale(hidden_one, gain_first)
    logits = jnp.dot(normed.astype(jnp.float32), router_weight, precision=lax.Precision.HIGHEST)
    router_probs = jax.nn.softmax(logits, axis=-1)
    picked = jnp.take_along_axis(router_probs, routes, axis=1)
    gate_weights = picked / jnp.sum(picked, axis=1, keepdims=True)
    flat_ids = routes.reshape(-1)
    expert_iota = jnp.arange(n_expert, dtype=jnp.int32)
    onehot = (flat_ids[:, None] == expert_iota[None, :]).astype(jnp.int32)
    earlier = jnp.cumsum(onehot, axis=0) - onehot
    slot_index = jnp.sum(earlier * onehot, axis=1)
    target = flat_ids * capacity + slot_index
    slot_iota = jnp.arange(n_expert * capacity, dtype=jnp.int32)
    placing = (slot_iota[:, None] == target[None, :]).astype(jnp.bfloat16)
    repeated = jnp.repeat(normed, 2, axis=0)
    send_slots = jnp.dot(placing, repeated, preferred_element_type=jnp.float32).astype(jnp.bfloat16)
    send_slots = send_slots.reshape(n_expert, capacity, width)
    received = lax.all_to_all(send_slots, "expert", split_axis=0, concat_axis=0, tiled=True)
    received, *pieces = lax.optimization_barrier((received, *pieces))
    weights = jnp.concatenate(pieces, axis=1)
    gate_rows, up_rows, down_rows = weights[0], weights[1], weights[2]
    slot_total = n_expert * capacity
    rows_in = received.reshape(slot_total, width)
    all_rows = [rows_in] + [lax.ppermute(rows_in, "ty", shift_pairs(n_ty, s)) for s in range(1, n_ty)]
    all_rows = jnp.concatenate(all_rows, axis=0)
    partial = expert_block(all_rows, gate_rows, up_rows, down_rows).astype(jnp.bfloat16)
    partial = partial.reshape(n_ty, slot_total, width)
    expert_sum = partial[0].astype(jnp.float32)
    for s in range(1, n_ty):
        back = lax.ppermute(partial[s], "ty", shift_pairs(n_ty, -s))
        expert_sum = expert_sum + back.astype(jnp.float32)
    expert_sum = expert_sum.astype(jnp.bfloat16)
    expert_out = expert_sum.reshape(n_expert, capacity, width)
    returned = lax.all_to_all(expert_out, "expert", split_axis=0, concat_axis=0, tiled=True)
    returned = returned.reshape(slot_total, width)
    per_route = lax.dot_general(
        placing, returned, (((0,), (0,)), ((), ())), preferred_element_type=jnp.float32
    )
    per_route = per_route.reshape(row_count, 2, width)
    mixed = jnp.sum(gate_weights[:, :, None] * per_route, axis=1)
    residual_out = (hidden_one.astype(jnp.float32) + mixed).astype(jnp.bfloat16)
    next_normed = rms_scale(residual_out, gain_second)
    return (residual_out, next_normed)


def shift_pairs(n, shift):
    return [(i, (i + shift) % n) for i in range(n)]


def split_tensor(n):
    inner = int(math.isqrt(n))
    while n % inner:
        inner -= 1
    return n // inner, inner


def solution(mesh):
    n_expert = mesh.shape["expert"]
    n_ty, n_tx = split_tensor(mesh.shape["tensor"])
    grid = Mesh(mesh.devices.reshape(n_expert, n_ty, n_tx), ROWS_AXES)
    rows = P(ROWS_AXES, None)
    placed = (
        rows,
        P(TENSOR_AXES, "expert"),
        P(TENSOR_AXES, None),
        P(),
        P(),
        rows,
        P("expert", TENSOR_AXES, None),
        P("expert", TENSOR_AXES, None),
        P("expert", TENSOR_AXES, None),
        P(),
    )
    return jax.shard_map(
        per_device,
        mesh=grid,
        in_specs=placed,
        out_specs=(rows, rows),
        check_vma=False,
    )
```

```python
import math

import jax
import jax.numpy as jnp
from jax import lax
from jax.sharding import Mesh
from jax.sharding import PartitionSpec as P

ROWS_AXES = ("expert", "ty", "tx")
TENSOR_AXES = ("ty", "tx")


def rms_scale(values, gain):
    wide = values.astype(jnp.float32)
    scale = lax.rsqrt(jnp.mean(wide * wide, axis=-1, keepdims=True) + 1e-06)
    return (wide * scale * gain).astype(jnp.bfloat16)


def expert_block(inputs, gate_rows, up_rows, down_rows):
    gate_part = lax.dot_general(
        inputs, gate_rows, (((1,), (1,)), ((), ())), preferred_element_type=jnp.float32
    )
    up_part = lax.dot_general(
        inputs, up_rows, (((1,), (1,)), ((), ())), preferred_element_type=jnp.float32
    )
    hid = (jax.nn.gelu(gate_part, approximate=True) * up_part).astype(jnp.bfloat16)
    return jnp.dot(hid, down_rows, preferred_element_type=jnp.float32)


def per_device(
    residual_in,
    attn_heads,
    out_proj,
    gain_first,
    router_weight,
    routes,
    w_gate,
    w_upward,
    w_downward,
    gain_second,
):
    row_count = residual_in.shape[0]
    width = residual_in.shape[1]
    n_expert = lax.axis_size("expert")
    capacity = 4 * row_count // n_expert

    n_ty = lax.axis_size("ty")
    n_tx = lax.axis_size("tx")
    ty = lax.axis_index("ty")
    tx = lax.axis_index("tx")
    core = lax.axis_index("expert") % 2
    half = width // 2
    my_cols = lax.dynamic_slice_in_dim(out_proj, core * half, half, axis=1)
    near = [my_cols] + [lax.ppermute(my_cols, "tx", shift_pairs(n_tx, s)) for s in range(1, n_tx)]
    near = jnp.stack(near)
    my_half = [near] + [lax.ppermute(near, "ty", shift_pairs(n_ty, s)) for s in range(1, n_ty)]
    my_half = jnp.stack(my_half)
    other_half = lax.ppermute(my_half, "expert", [(i, i ^ 1) for i in range(n_expert)])
    own_heads = lax.all_to_all(attn_heads, TENSOR_AXES, 1, 0, tiled=True)
    own_heads = own_heads.reshape(n_ty, n_tx, -1, row_count)
    from_y = (ty - jnp.arange(n_ty)) % n_ty
    from_x = (tx - jnp.arange(n_tx)) % n_tx
    own_heads = jnp.take(jnp.take(own_heads, from_y, axis=0), from_x, axis=1)
    contract = (((0, 1, 2), (0, 1, 2)), ((), ()))
    proj_mine = lax.dot_general(own_heads, my_half, contract, preferred_element_type=jnp.float32)
    proj_other = lax.dot_general(own_heads, other_half, contract, preferred_element_type=jnp.float32)
    projected = jnp.where(
        core == 0,
        jnp.concatenate([proj_mine, proj_other], axis=1),
        jnp.concatenate([proj_other, proj_mine], axis=1),
    )

    stacked = jnp.concatenate([w_gate, w_upward, w_downward], axis=0)
    pieces = [stacked] + [
        lax.ppermute(stacked, "tx", shift_pairs(n_tx, s)) for s in range(1, n_tx)
    ]

    hidden_one = (residual_in.astype(jnp.float32) + projected).astype(jnp.bfloat16)
    normed = rms_scale(hidden_one, gain_first)
    logits = jnp.dot(normed.astype(jnp.float32), router_weight, precision=lax.Precision.HIGHEST)
    router_probs = jax.nn.softmax(logits, axis=-1)
    picked = jnp.take_along_axis(router_probs, routes, axis=1)
    gate_weights = picked / jnp.sum(picked, axis=1, keepdims=True)
    flat_ids = routes.reshape(-1)
    expert_iota = jnp.arange(n_expert, dtype=jnp.int32)
    onehot = (flat_ids[:, None] == expert_iota[None, :]).astype(jnp.int32)
    earlier = jnp.cumsum(onehot, axis=0) - onehot
    slot_index = jnp.sum(earlier * onehot, axis=1)
    target = flat_ids * capacity + slot_index
    slot_iota = jnp.arange(n_expert * capacity, dtype=jnp.int32)
    placing = (slot_iota[:, None] == target[None, :]).astype(jnp.bfloat16)
    repeated = jnp.repeat(normed, 2, axis=0)
    send_slots = jnp.dot(placing, repeated, preferred_element_type=jnp.float32).astype(jnp.bfloat16)
    send_slots = send_slots.reshape(n_expert, capacity, width)
    received = lax.all_to_all(send_slots, "expert", split_axis=0, concat_axis=0, tiled=True)
    weights = jnp.concatenate(pieces, axis=1)
    gate_rows, up_rows, down_rows = weights[0], weights[1], weights[2]
    slot_total = n_expert * capacity
    rows_in = received.reshape(slot_total, width)
    all_rows = [rows_in] + [lax.ppermute(rows_in, "ty", shift_pairs(n_ty, s)) for s in range(1, n_ty)]
    all_rows = jnp.concatenate(all_rows, axis=0)
    partial = expert_block(all_rows, gate_rows, up_rows, down_rows).astype(jnp.bfloat16)
    partial = partial.reshape(n_ty, slot_total, width)
    expert_sum = partial[0].astype(jnp.float32)
    for s in range(1, n_ty):
        back = lax.ppermute(partial[s], "ty", shift_pairs(n_ty, -s))
        expert_sum = expert_sum + back.astype(jnp.float32)
    expert_sum = expert_sum.astype(jnp.bfloat16)
    expert_out = expert_sum.reshape(n_expert, capacity, width)
    returned = lax.all_to_all(expert_out, "expert", split_axis=0, concat_axis=0, tiled=True)
    returned = returned.reshape(slot_total, width)
    per_route = lax.dot_general(
        placing, returned, (((0,), (0,)), ((), ())), preferred_element_type=jnp.float32
    )
    per_route = per_route.reshape(row_count, 2, width)
    mixed = jnp.sum(gate_weights[:, :, None] * per_route, axis=1)
    residual_out = (hidden_one.astype(jnp.float32) + mixed).astype(jnp.bfloat16)
    next_normed = rms_scale(residual_out, gain_second)
    return (residual_out, next_normed)


def shift_pairs(n, shift):
    return [(i, (i + shift) % n) for i in range(n)]


def split_tensor(n):
    inner = int(math.isqrt(n))
    while n % inner:
        inner -= 1
    return n // inner, inner


def solution(mesh):
    n_expert = mesh.shape["expert"]
    n_ty, n_tx = split_tensor(mesh.shape["tensor"])
    grid = Mesh(mesh.devices.reshape(n_expert, n_ty, n_tx), ROWS_AXES)
    rows = P(ROWS_AXES, None)
    placed = (
        rows,
        P(TENSOR_AXES, "expert"),
        P(TENSOR_AXES, None),
        P(),
        P(),
        rows,
        P("expert", TENSOR_AXES, None),
        P("expert", TENSOR_AXES, None),
        P("expert", TENSOR_AXES, None),
        P(),
    )
    return jax.shard_map(
        per_device,
        mesh=grid,
        in_specs=placed,
        out_specs=(rows, rows),
        check_vma=False,
    )
```

```python
import math

import jax
import jax.numpy as jnp
from jax import lax
from jax.sharding import Mesh
from jax.sharding import PartitionSpec as P

ROWS_AXES = ("expert", "ty", "tx")
TENSOR_AXES = ("ty", "tx")


def rms_scale(values, gain):
    wide = values.astype(jnp.float32)
    scale = lax.rsqrt(jnp.mean(wide * wide, axis=-1, keepdims=True) + 1e-06)
    return (wide * scale * gain).astype(jnp.bfloat16)


def expert_block(inputs, gate_rows, up_rows, down_rows):
    gate_part = lax.dot_general(
        inputs, gate_rows, (((1,), (1,)), ((), ())), preferred_element_type=jnp.float32
    )
    up_part = lax.dot_general(
        inputs, up_rows, (((1,), (1,)), ((), ())), preferred_element_type=jnp.float32
    )
    hid = (jax.nn.gelu(gate_part, approximate=True) * up_part).astype(jnp.bfloat16)
    return jnp.dot(hid, down_rows, preferred_element_type=jnp.float32)


def per_device(
    residual_in,
    attn_heads,
    out_proj,
    gain_first,
    router_weight,
    routes,
    w_gate,
    w_upward,
    w_downward,
    gain_second,
):
    row_count = residual_in.shape[0]
    width = residual_in.shape[1]
    n_expert = lax.axis_size("expert")
    capacity = 4 * row_count // n_expert

    n_ty = lax.axis_size("ty")
    n_tx = lax.axis_size("tx")
    ty = lax.axis_index("ty")
    tx = lax.axis_index("tx")
    core = lax.axis_index("expert") % 2
    half = width // 2
    my_cols = lax.dynamic_slice_in_dim(out_proj, core * half, half, axis=1)
    near = [my_cols] + [lax.ppermute(my_cols, "tx", shift_pairs(n_tx, s)) for s in range(1, n_tx)]
    near = jnp.stack(near)
    my_half = [near] + [lax.ppermute(near, "ty", shift_pairs(n_ty, s)) for s in range(1, n_ty)]
    my_half = jnp.stack(my_half)
    other_half = lax.ppermute(my_half, "expert", [(i, i ^ 1) for i in range(n_expert)])
    own_heads = lax.all_to_all(attn_heads, TENSOR_AXES, 1, 0, tiled=True)
    own_heads = own_heads.reshape(n_ty, n_tx, -1, row_count)
    from_y = (ty - jnp.arange(n_ty)) % n_ty
    from_x = (tx - jnp.arange(n_tx)) % n_tx
    own_heads = jnp.take(jnp.take(own_heads, from_y, axis=0), from_x, axis=1)
    contract = (((0, 1, 2), (0, 1, 2)), ((), ()))
    proj_mine = lax.dot_general(own_heads, my_half, contract, preferred_element_type=jnp.float32)
    proj_other = lax.dot_general(own_heads, other_half, contract, preferred_element_type=jnp.float32)
    projected = jnp.where(
        core == 0,
        jnp.concatenate([proj_mine, proj_other], axis=1),
        jnp.concatenate([proj_other, proj_mine], axis=1),
    )

    stacked = jnp.concatenate([w_gate, w_upward, w_downward], axis=0)
    pieces = [stacked] + [
        lax.ppermute(stacked, "tx", shift_pairs(n_tx, s)) for s in range(1, n_tx)
    ]

    hidden_one = (residual_in.astype(jnp.float32) + projected).astype(jnp.bfloat16)
    normed = rms_scale(hidden_one, gain_first)
    logits = jnp.dot(normed.astype(jnp.float32), router_weight, precision=lax.Precision.HIGHEST)
    router_probs = jax.nn.softmax(logits, axis=-1)
    picked = jnp.take_along_axis(router_probs, routes, axis=1)
    gate_weights = picked / jnp.sum(picked, axis=1, keepdims=True)
    flat_ids = routes.reshape(-1)
    expert_iota = jnp.arange(n_expert, dtype=jnp.int32)
    onehot = (flat_ids[:, None] == expert_iota[None, :]).astype(jnp.int32)
    earlier = jnp.cumsum(onehot, axis=0) - onehot
    slot_index = jnp.sum(earlier * onehot, axis=1)
    target = flat_ids * capacity + slot_index
    slot_iota = jnp.arange(n_expert * capacity, dtype=jnp.int32)
    placing = (slot_iota[:, None] == target[None, :]).astype(jnp.bfloat16)
    repeated = jnp.repeat(normed, 2, axis=0)
    send_slots = jnp.dot(placing, repeated, preferred_element_type=jnp.float32).astype(jnp.bfloat16)
    send_slots = send_slots.reshape(n_expert, capacity, width)
    slot_total = n_expert * capacity
    n_chunks = 2
    chunk = capacity // n_chunks
    weights = jnp.concatenate(pieces, axis=1)
    gate_rows, up_rows, down_rows = weights[0], weights[1], weights[2]
    returned = []
    for c in range(n_chunks):
        part = send_slots[:, c * chunk:(c + 1) * chunk]
        received = lax.all_to_all(part, "expert", split_axis=0, concat_axis=0, tiled=True)
        rows_in = received.reshape(n_expert * chunk, width)
        all_rows = [rows_in] + [
            lax.ppermute(rows_in, "ty", shift_pairs(n_ty, s)) for s in range(1, n_ty)
        ]
        all_rows = jnp.concatenate(all_rows, axis=0)
        partial = expert_block(all_rows, gate_rows, up_rows, down_rows).astype(jnp.bfloat16)
        partial = partial.reshape(n_ty, n_expert * chunk, width)
        expert_sum = partial[0].astype(jnp.float32)
        for s in range(1, n_ty):
            back = lax.ppermute(partial[s], "ty", shift_pairs(n_ty, -s))
            expert_sum = expert_sum + back.astype(jnp.float32)
        expert_out = expert_sum.astype(jnp.bfloat16).reshape(n_expert, chunk, width)
        returned.append(lax.all_to_all(expert_out, "expert", split_axis=0, concat_axis=0, tiled=True))
    returned = jnp.concatenate(returned, axis=1).reshape(slot_total, width)
    per_route = lax.dot_general(
        placing, returned, (((0,), (0,)), ((), ())), preferred_element_type=jnp.float32
    )
    per_route = per_route.reshape(row_count, 2, width)
    mixed = jnp.sum(gate_weights[:, :, None] * per_route, axis=1)
    residual_out = (hidden_one.astype(jnp.float32) + mixed).astype(jnp.bfloat16)
    next_normed = rms_scale(residual_out, gain_second)
    return (residual_out, next_normed)


def shift_pairs(n, shift):
    return [(i, (i + shift) % n) for i in range(n)]


def split_tensor(n):
    inner = int(math.isqrt(n))
    while n % inner:
        inner -= 1
    return n // inner, inner


def solution(mesh):
    n_expert = mesh.shape["expert"]
    n_ty, n_tx = split_tensor(mesh.shape["tensor"])
    grid = Mesh(mesh.devices.reshape(n_expert, n_ty, n_tx), ROWS_AXES)
    rows = P(ROWS_AXES, None)
    placed = (
        rows,
        P(TENSOR_AXES, "expert"),
        P(TENSOR_AXES, None),
        P(),
        P(),
        rows,
        P("expert", TENSOR_AXES, None),
        P("expert", TENSOR_AXES, None),
        P("expert", TENSOR_AXES, None),
        P(),
    )
    return jax.shard_map(
        per_device,
        mesh=grid,
        in_specs=placed,
        out_specs=(rows, rows),
        check_vma=False,
    )
```

```python
import math

import jax
import jax.numpy as jnp
from jax import lax
from jax.sharding import Mesh
from jax.sharding import PartitionSpec as P

ROWS_AXES = ("expert", "ty", "tx")
TENSOR_AXES = ("ty", "tx")


def rms_scale(values, gain):
    wide = values.astype(jnp.float32)
    scale = lax.rsqrt(jnp.mean(wide * wide, axis=-1, keepdims=True) + 1e-06)
    return (wide * scale * gain).astype(jnp.bfloat16)


def expert_block(inputs, gate_rows, up_rows, down_rows):
    gate_part = lax.dot_general(
        inputs, gate_rows, (((1,), (1,)), ((), ())), preferred_element_type=jnp.float32
    )
    up_part = lax.dot_general(
        inputs, up_rows, (((1,), (1,)), ((), ())), preferred_element_type=jnp.float32
    )
    hid = (jax.nn.gelu(gate_part, approximate=True) * up_part).astype(jnp.bfloat16)
    return jnp.dot(hid, down_rows, preferred_element_type=jnp.float32)


def per_device(
    residual_in,
    attn_heads,
    out_proj,
    gain_first,
    router_weight,
    routes,
    w_gate,
    w_upward,
    w_downward,
    gain_second,
):
    row_count = residual_in.shape[0]
    width = residual_in.shape[1]
    n_expert = lax.axis_size("expert")
    capacity = 4 * row_count // n_expert

    n_ty = lax.axis_size("ty")
    n_tx = lax.axis_size("tx")
    ty = lax.axis_index("ty")
    tx = lax.axis_index("tx")
    core = lax.axis_index("expert") % 2
    half = width // 2
    my_cols = lax.dynamic_slice_in_dim(out_proj, core * half, half, axis=1)
    n_tensor = n_ty * n_tx
    heads_for = attn_heads.reshape(-1, n_tensor, row_count).transpose(1, 0, 2)
    proj_for = jnp.broadcast_to(my_cols, (n_tensor, *my_cols.shape))
    mail = jnp.concatenate([heads_for, proj_for], axis=2)
    mail = lax.all_to_all(mail, TENSOR_AXES, 0, 0, tiled=True)
    own_heads = mail[:, :, :row_count]
    my_half = mail[:, :, row_count:]
    other_half = lax.ppermute(my_half, "expert", [(i, i ^ 1) for i in range(n_expert)])
    contract = (((0, 1), (0, 1)), ((), ()))
    proj_mine = lax.dot_general(own_heads, my_half, contract, preferred_element_type=jnp.float32)
    proj_other = lax.dot_general(own_heads, other_half, contract, preferred_element_type=jnp.float32)
    projected = jnp.where(
        core == 0,
        jnp.concatenate([proj_mine, proj_other], axis=1),
        jnp.concatenate([proj_other, proj_mine], axis=1),
    )

    stacked = jnp.concatenate([w_gate, w_upward, w_downward], axis=0)
    pieces = [stacked] + [
        lax.ppermute(stacked, "tx", shift_pairs(n_tx, s)) for s in range(1, n_tx)
    ]

    hidden_one = (residual_in.astype(jnp.float32) + projected).astype(jnp.bfloat16)
    normed = rms_scale(hidden_one, gain_first)
    logits = jnp.dot(normed.astype(jnp.float32), router_weight, precision=lax.Precision.HIGHEST)
    router_probs = jax.nn.softmax(logits, axis=-1)
    picked = jnp.take_along_axis(router_probs, routes, axis=1)
    gate_weights = picked / jnp.sum(picked, axis=1, keepdims=True)
    flat_ids = routes.reshape(-1)
    expert_iota = jnp.arange(n_expert, dtype=jnp.int32)
    onehot = (flat_ids[:, None] == expert_iota[None, :]).astype(jnp.int32)
    earlier = jnp.cumsum(onehot, axis=0) - onehot
    slot_index = jnp.sum(earlier * onehot, axis=1)
    target = flat_ids * capacity + slot_index
    slot_iota = jnp.arange(n_expert * capacity, dtype=jnp.int32)
    placing = (slot_iota[:, None] == target[None, :]).astype(jnp.bfloat16)
    repeated = jnp.repeat(normed, 2, axis=0)
    send_slots = jnp.dot(placing, repeated, preferred_element_type=jnp.float32).astype(jnp.bfloat16)
    send_slots = send_slots.reshape(n_expert, capacity, width)
    received = lax.all_to_all(send_slots, "expert", split_axis=0, concat_axis=0, tiled=True)
    weights = jnp.concatenate(pieces, axis=1)
    gate_rows, up_rows, down_rows = weights[0], weights[1], weights[2]
    slot_total = n_expert * capacity
    rows_in = received.reshape(slot_total, width)
    all_rows = [rows_in] + [lax.ppermute(rows_in, "ty", shift_pairs(n_ty, s)) for s in range(1, n_ty)]
    all_rows = jnp.concatenate(all_rows, axis=0)
    partial = expert_block(all_rows, gate_rows, up_rows, down_rows).astype(jnp.bfloat16)
    partial = partial.reshape(n_ty, slot_total, width)
    expert_sum = partial[0].astype(jnp.float32)
    for s in range(1, n_ty):
        back = lax.ppermute(partial[s], "ty", shift_pairs(n_ty, -s))
        expert_sum = expert_sum + back.astype(jnp.float32)
    expert_sum = expert_sum.astype(jnp.bfloat16)
    expert_out = expert_sum.reshape(n_expert, capacity, width)
    returned = lax.all_to_all(expert_out, "expert", split_axis=0, concat_axis=0, tiled=True)
    returned = returned.reshape(slot_total, width)
    per_route = lax.dot_general(
        placing, returned, (((0,), (0,)), ((), ())), preferred_element_type=jnp.float32
    )
    per_route = per_route.reshape(row_count, 2, width)
    mixed = jnp.sum(gate_weights[:, :, None] * per_route, axis=1)
    residual_out = (hidden_one.astype(jnp.float32) + mixed).astype(jnp.bfloat16)
    next_normed = rms_scale(residual_out, gain_second)
    return (residual_out, next_normed)


def shift_pairs(n, shift):
    return [(i, (i + shift) % n) for i in range(n)]


def split_tensor(n):
    inner = int(math.isqrt(n))
    while n % inner:
        inner -= 1
    return n // inner, inner


def solution(mesh):
    n_expert = mesh.shape["expert"]
    n_ty, n_tx = split_tensor(mesh.shape["tensor"])
    grid = Mesh(mesh.devices.reshape(n_expert, n_ty, n_tx), ROWS_AXES)
    rows = P(ROWS_AXES, None)
    placed = (
        rows,
        P(TENSOR_AXES, "expert"),
        P(TENSOR_AXES, None),
        P(),
        P(),
        rows,
        P("expert", TENSOR_AXES, None),
        P("expert", TENSOR_AXES, None),
        P("expert", TENSOR_AXES, None),
        P(),
    )
    return jax.shard_map(
        per_device,
        mesh=grid,
        in_specs=placed,
        out_specs=(rows, rows),
        check_vma=False,
    )
```

```python
import math

import jax
import jax.numpy as jnp
from jax import lax
from jax.sharding import Mesh
from jax.sharding import PartitionSpec as P

EXPERT_AXES = ("ez", "ec")
ROWS_AXES = ("ez", "ec", "ty", "tx")
TENSOR_AXES = ("ty", "tx")


def rms_scale(values, gain):
    wide = values.astype(jnp.float32)
    scale = lax.rsqrt(jnp.mean(wide * wide, axis=-1, keepdims=True) + 1e-06)
    return (wide * scale * gain).astype(jnp.bfloat16)


def expert_block(inputs, gate_rows, up_rows, down_rows):
    gate_part = lax.dot_general(
        inputs, gate_rows, (((1,), (1,)), ((), ())), preferred_element_type=jnp.float32
    )
    up_part = lax.dot_general(
        inputs, up_rows, (((1,), (1,)), ((), ())), preferred_element_type=jnp.float32
    )
    hid = (jax.nn.gelu(gate_part, approximate=True) * up_part).astype(jnp.bfloat16)
    return jnp.dot(hid, down_rows, preferred_element_type=jnp.float32)


def per_device(
    residual_in,
    attn_heads,
    out_proj,
    gain_first,
    router_weight,
    routes,
    w_gate,
    w_upward,
    w_downward,
    gain_second,
):
    row_count = residual_in.shape[0]
    width = residual_in.shape[1]
    n_ez = lax.axis_size("ez")
    n_ec = lax.axis_size("ec")
    n_expert = n_ez * n_ec
    capacity = 4 * row_count // n_expert

    n_ty = lax.axis_size("ty")
    n_tx = lax.axis_size("tx")
    ty = lax.axis_index("ty")
    tx = lax.axis_index("tx")
    core = lax.axis_index("ec")
    half = width // 2
    my_cols = lax.dynamic_slice_in_dim(out_proj, core * half, half, axis=1)
    near = [my_cols] + [lax.ppermute(my_cols, "tx", shift_pairs(n_tx, s)) for s in range(1, n_tx)]
    near = jnp.stack(near)
    my_half = [near] + [lax.ppermute(near, "ty", shift_pairs(n_ty, s)) for s in range(1, n_ty)]
    my_half = jnp.stack(my_half)
    other_half = lax.ppermute(my_half, "ec", [(i, i ^ 1) for i in range(n_ec)])
    own_heads = lax.all_to_all(attn_heads, TENSOR_AXES, 1, 0, tiled=True)
    own_heads = own_heads.reshape(n_ty, n_tx, -1, row_count)
    from_y = (ty - jnp.arange(n_ty)) % n_ty
    from_x = (tx - jnp.arange(n_tx)) % n_tx
    own_heads = jnp.take(jnp.take(own_heads, from_y, axis=0), from_x, axis=1)
    contract = (((0, 1, 2), (0, 1, 2)), ((), ()))
    proj_mine = lax.dot_general(own_heads, my_half, contract, preferred_element_type=jnp.float32)
    proj_other = lax.dot_general(own_heads, other_half, contract, preferred_element_type=jnp.float32)
    projected = jnp.where(
        core == 0,
        jnp.concatenate([proj_mine, proj_other], axis=1),
        jnp.concatenate([proj_other, proj_mine], axis=1),
    )

    stacked = jnp.concatenate([w_gate, w_upward, w_downward], axis=0)
    pieces = [stacked] + [
        lax.ppermute(stacked, "tx", shift_pairs(n_tx, s)) for s in range(1, n_tx)
    ]

    hidden_one = (residual_in.astype(jnp.float32) + projected).astype(jnp.bfloat16)
    normed = rms_scale(hidden_one, gain_first)
    logits = jnp.dot(normed.astype(jnp.float32), router_weight, precision=lax.Precision.HIGHEST)
    router_probs = jax.nn.softmax(logits, axis=-1)
    picked = jnp.take_along_axis(router_probs, routes, axis=1)
    gate_weights = picked / jnp.sum(picked, axis=1, keepdims=True)
    flat_ids = routes.reshape(-1)
    expert_iota = jnp.arange(n_expert, dtype=jnp.int32)
    onehot = (flat_ids[:, None] == expert_iota[None, :]).astype(jnp.int32)
    earlier = jnp.cumsum(onehot, axis=0) - onehot
    slot_index = jnp.sum(earlier * onehot, axis=1)
    target = flat_ids * capacity + slot_index
    slot_iota = jnp.arange(n_expert * capacity, dtype=jnp.int32)
    placing = (slot_iota[:, None] == target[None, :]).astype(jnp.bfloat16)
    repeated = jnp.repeat(normed, 2, axis=0)
    send_slots = jnp.dot(placing, repeated, preferred_element_type=jnp.float32).astype(jnp.bfloat16)
    send_slots = send_slots.reshape(n_expert, capacity, width)
    send_slots = send_slots.reshape(n_ez, n_ec, capacity, width)
    received = lax.all_to_all(send_slots, "ez", split_axis=0, concat_axis=0, tiled=True)
    received = lax.all_to_all(received, "ec", split_axis=1, concat_axis=1, tiled=True)
    weights = jnp.concatenate(pieces, axis=1)
    gate_rows, up_rows, down_rows = weights[0], weights[1], weights[2]
    slot_total = n_expert * capacity
    rows_in = received.reshape(slot_total, width)
    all_rows = [rows_in] + [lax.ppermute(rows_in, "ty", shift_pairs(n_ty, s)) for s in range(1, n_ty)]
    all_rows = jnp.concatenate(all_rows, axis=0)
    partial = expert_block(all_rows, gate_rows, up_rows, down_rows).astype(jnp.bfloat16)
    partial = partial.reshape(n_ty, slot_total, width)
    expert_sum = partial[0].astype(jnp.float32)
    for s in range(1, n_ty):
        back = lax.ppermute(partial[s], "ty", shift_pairs(n_ty, -s))
        expert_sum = expert_sum + back.astype(jnp.float32)
    expert_sum = expert_sum.astype(jnp.bfloat16)
    expert_out = expert_sum.reshape(n_ez, n_ec, capacity, width)
    returned = lax.all_to_all(expert_out, "ec", split_axis=1, concat_axis=1, tiled=True)
    returned = lax.all_to_all(returned, "ez", split_axis=0, concat_axis=0, tiled=True)
    returned = returned.reshape(slot_total, width)
    per_route = lax.dot_general(
        placing, returned, (((0,), (0,)), ((), ())), preferred_element_type=jnp.float32
    )
    per_route = per_route.reshape(row_count, 2, width)
    mixed = jnp.sum(gate_weights[:, :, None] * per_route, axis=1)
    residual_out = (hidden_one.astype(jnp.float32) + mixed).astype(jnp.bfloat16)
    next_normed = rms_scale(residual_out, gain_second)
    return (residual_out, next_normed)


def shift_pairs(n, shift):
    return [(i, (i + shift) % n) for i in range(n)]


def split_tensor(n):
    inner = int(math.isqrt(n))
    while n % inner:
        inner -= 1
    return n // inner, inner


def solution(mesh):
    n_expert = mesh.shape["expert"]
    n_ty, n_tx = split_tensor(mesh.shape["tensor"])
    n_ec = 2 if n_expert % 2 == 0 else 1
    grid = Mesh(mesh.devices.reshape(n_expert // n_ec, n_ec, n_ty, n_tx), ROWS_AXES)
    rows = P(ROWS_AXES, None)
    placed = (
        rows,
        P(TENSOR_AXES, EXPERT_AXES),
        P(TENSOR_AXES, None),
        P(),
        P(),
        rows,
        P(EXPERT_AXES, TENSOR_AXES, None),
        P(EXPERT_AXES, TENSOR_AXES, None),
        P(EXPERT_AXES, TENSOR_AXES, None),
        P(),
    )
    return jax.shard_map(
        per_device,
        mesh=grid,
        in_specs=placed,
        out_specs=(rows, rows),
        check_vma=False,
    )
```

```python
import math

import jax
import jax.numpy as jnp
from jax import lax
from jax.sharding import Mesh
from jax.sharding import PartitionSpec as P

ROWS_AXES = ("expert", "ty", "tx")
TENSOR_AXES = ("ty", "tx")


def rms_scale(values, gain):
    wide = values.astype(jnp.float32)
    scale = lax.rsqrt(jnp.mean(wide * wide, axis=-1, keepdims=True) + 1e-06)
    return (wide * scale * gain).astype(jnp.bfloat16)


def expert_block(inputs, gate_rows, up_rows, down_rows):
    gate_part = lax.dot_general(
        inputs, gate_rows, (((1,), (1,)), ((), ())), preferred_element_type=jnp.float32
    )
    up_part = lax.dot_general(
        inputs, up_rows, (((1,), (1,)), ((), ())), preferred_element_type=jnp.float32
    )
    hid = (jax.nn.gelu(gate_part, approximate=True) * up_part).astype(jnp.bfloat16)
    return jnp.dot(hid, down_rows, preferred_element_type=jnp.float32)


def per_device(
    residual_in,
    attn_heads,
    out_proj,
    gain_first,
    router_weight,
    routes,
    w_gate,
    w_upward,
    w_downward,
    gain_second,
):
    row_count = residual_in.shape[0]
    width = residual_in.shape[1]
    n_expert = lax.axis_size("expert")
    capacity = 4 * row_count // n_expert

    n_ty = lax.axis_size("ty")
    n_tx = lax.axis_size("tx")
    ty = lax.axis_index("ty")
    tx = lax.axis_index("tx")
    core = lax.axis_index("expert") % 2
    half = width // 2
    my_cols = lax.dynamic_slice_in_dim(out_proj, core * half, half, axis=1)
    near = [my_cols] + [lax.ppermute(my_cols, "tx", shift_pairs(n_tx, s)) for s in range(1, n_tx)]
    near = jnp.stack(near)
    my_half = [near] + [lax.ppermute(near, "ty", shift_pairs(n_ty, s)) for s in range(1, n_ty)]
    my_half = jnp.stack(my_half)
    other_half = lax.ppermute(my_half, "expert", [(i, i ^ 1) for i in range(n_expert)])
    own_heads = lax.all_to_all(attn_heads, TENSOR_AXES, 1, 0, tiled=True)
    own_heads = own_heads.reshape(n_ty, n_tx, -1, row_count)
    from_y = (ty - jnp.arange(n_ty)) % n_ty
    from_x = (tx - jnp.arange(n_tx)) % n_tx
    own_heads = jnp.take(jnp.take(own_heads, from_y, axis=0), from_x, axis=1)
    contract = (((0, 1, 2), (0, 1, 2)), ((), ()))
    proj_mine = lax.dot_general(own_heads, my_half, contract, preferred_element_type=jnp.float32)
    proj_other = lax.dot_general(own_heads, other_half, contract, preferred_element_type=jnp.float32)
    projected = jnp.where(
        core == 0,
        jnp.concatenate([proj_mine, proj_other], axis=1),
        jnp.concatenate([proj_other, proj_mine], axis=1),
    )

    stacked = jnp.concatenate([w_gate, w_upward, w_downward], axis=0)
    pieces = [stacked] + [
        lax.ppermute(stacked, "ty", shift_pairs(n_ty, s)) for s in range(1, n_ty)
    ]

    hidden_one = (residual_in.astype(jnp.float32) + projected).astype(jnp.bfloat16)
    normed = rms_scale(hidden_one, gain_first)
    logits = jnp.dot(normed.astype(jnp.float32), router_weight, precision=lax.Precision.HIGHEST)
    router_probs = jax.nn.softmax(logits, axis=-1)
    picked = jnp.take_along_axis(router_probs, routes, axis=1)
    gate_weights = picked / jnp.sum(picked, axis=1, keepdims=True)
    flat_ids = routes.reshape(-1)
    expert_iota = jnp.arange(n_expert, dtype=jnp.int32)
    onehot = (flat_ids[:, None] == expert_iota[None, :]).astype(jnp.int32)
    earlier = jnp.cumsum(onehot, axis=0) - onehot
    slot_index = jnp.sum(earlier * onehot, axis=1)
    target = flat_ids * capacity + slot_index
    slot_iota = jnp.arange(n_expert * capacity, dtype=jnp.int32)
    placing = (slot_iota[:, None] == target[None, :]).astype(jnp.bfloat16)
    repeated = jnp.repeat(normed, 2, axis=0)
    send_slots = jnp.dot(placing, repeated, preferred_element_type=jnp.float32).astype(jnp.bfloat16)
    send_slots = send_slots.reshape(n_expert, capacity, width)
    received = lax.all_to_all(send_slots, "expert", split_axis=0, concat_axis=0, tiled=True)
    weights = jnp.concatenate(pieces, axis=1)
    gate_rows, up_rows, down_rows = weights[0], weights[1], weights[2]
    slot_total = n_expert * capacity
    rows_in = received.reshape(slot_total, width)
    all_rows = [rows_in] + [lax.ppermute(rows_in, "tx", shift_pairs(n_tx, s)) for s in range(1, n_tx)]
    all_rows = jnp.concatenate(all_rows, axis=0)
    partial = expert_block(all_rows, gate_rows, up_rows, down_rows).astype(jnp.bfloat16)
    partial = partial.reshape(n_tx, slot_total, width)
    expert_sum = partial[0].astype(jnp.float32)
    for s in range(1, n_tx):
        back = lax.ppermute(partial[s], "tx", shift_pairs(n_tx, -s))
        expert_sum = expert_sum + back.astype(jnp.float32)
    expert_sum = expert_sum.astype(jnp.bfloat16)
    expert_out = expert_sum.reshape(n_expert, capacity, width)
    returned = lax.all_to_all(expert_out, "expert", split_axis=0, concat_axis=0, tiled=True)
    returned = returned.reshape(slot_total, width)
    per_route = lax.dot_general(
        placing, returned, (((0,), (0,)), ((), ())), preferred_element_type=jnp.float32
    )
    per_route = per_route.reshape(row_count, 2, width)
    mixed = jnp.sum(gate_weights[:, :, None] * per_route, axis=1)
    residual_out = (hidden_one.astype(jnp.float32) + mixed).astype(jnp.bfloat16)
    next_normed = rms_scale(residual_out, gain_second)
    return (residual_out, next_normed)


def shift_pairs(n, shift):
    return [(i, (i + shift) % n) for i in range(n)]


def split_tensor(n):
    inner = int(math.isqrt(n))
    while n % inner:
        inner -= 1
    return n // inner, inner


def solution(mesh):
    n_expert = mesh.shape["expert"]
    n_ty, n_tx = split_tensor(mesh.shape["tensor"])
    grid = Mesh(mesh.devices.reshape(n_expert, n_ty, n_tx), ROWS_AXES)
    rows = P(ROWS_AXES, None)
    placed = (
        rows,
        P(TENSOR_AXES, "expert"),
        P(TENSOR_AXES, None),
        P(),
        P(),
        rows,
        P("expert", TENSOR_AXES, None),
        P("expert", TENSOR_AXES, None),
        P("expert", TENSOR_AXES, None),
        P(),
    )
    return jax.shard_map(
        per_device,
        mesh=grid,
        in_specs=placed,
        out_specs=(rows, rows),
        check_vma=False,
    )
```

```python
import math

import jax
import jax.numpy as jnp
from jax import lax
from jax.sharding import Mesh
from jax.sharding import PartitionSpec as P

ROWS_AXES = ("expert", "ty", "tx")
TENSOR_AXES = ("ty", "tx")


def rms_scale(values, gain):
    wide = values.astype(jnp.float32)
    scale = lax.rsqrt(jnp.mean(wide * wide, axis=-1, keepdims=True) + 1e-06)
    return (wide * scale * gain).astype(jnp.bfloat16)


def expert_block(inputs, gate_rows, up_rows, down_rows):
    gate_part = lax.dot_general(
        inputs, gate_rows, (((1,), (1,)), ((), ())), preferred_element_type=jnp.float32
    )
    up_part = lax.dot_general(
        inputs, up_rows, (((1,), (1,)), ((), ())), preferred_element_type=jnp.float32
    )
    hid = (jax.nn.gelu(gate_part, approximate=True) * up_part).astype(jnp.bfloat16)
    return jnp.dot(hid, down_rows, preferred_element_type=jnp.float32)


def per_device(
    residual_in,
    attn_heads,
    out_proj,
    gain_first,
    router_weight,
    routes,
    w_gate,
    w_upward,
    w_downward,
    gain_second,
):
    row_count = residual_in.shape[0]
    width = residual_in.shape[1]
    n_expert = lax.axis_size("expert")
    capacity = 4 * row_count // n_expert

    n_ty = lax.axis_size("ty")
    n_tx = lax.axis_size("tx")
    ty = lax.axis_index("ty")
    tx = lax.axis_index("tx")
    core = lax.axis_index("expert") % 2
    half = width // 2
    my_cols = lax.dynamic_slice_in_dim(out_proj, core * half, half, axis=1)
    near = [my_cols] + [lax.ppermute(my_cols, "tx", shift_pairs(n_tx, s)) for s in range(1, n_tx)]
    near = jnp.stack(near)
    my_half = [near] + [lax.ppermute(near, "ty", shift_pairs(n_ty, s)) for s in range(1, n_ty)]
    my_half = jnp.stack(my_half)
    other_half = lax.ppermute(my_half, "expert", [(i, i ^ 1) for i in range(n_expert)])
    own_heads = lax.all_to_all(attn_heads, TENSOR_AXES, 1, 0, tiled=True)
    own_heads = own_heads.reshape(n_ty, n_tx, -1, row_count)
    from_y = (ty - jnp.arange(n_ty)) % n_ty
    from_x = (tx - jnp.arange(n_tx)) % n_tx
    own_heads = jnp.take(jnp.take(own_heads, from_y, axis=0), from_x, axis=1)
    contract = (((0, 1, 2), (0, 1, 2)), ((), ()))
    proj_mine = lax.dot_general(own_heads, my_half, contract, preferred_element_type=jnp.float32)
    proj_other = lax.dot_general(own_heads, other_half, contract, preferred_element_type=jnp.float32)
    projected = jnp.where(
        core == 0,
        jnp.concatenate([proj_mine, proj_other], axis=1),
        jnp.concatenate([proj_other, proj_mine], axis=1),
    )

    stacked = jnp.concatenate([w_gate, w_upward, w_downward], axis=0)
    pieces = [stacked] + [
        lax.ppermute(stacked, "ty", shift_pairs(n_ty, s)) for s in range(1, n_ty)
    ]

    hidden_one = (residual_in.astype(jnp.float32) + projected).astype(jnp.bfloat16)
    normed = rms_scale(hidden_one, gain_first)
    logits = jnp.dot(normed.astype(jnp.float32), router_weight, precision=lax.Precision.HIGHEST)
    router_probs = jax.nn.softmax(logits, axis=-1)
    picked = jnp.take_along_axis(router_probs, routes, axis=1)
    gate_weights = picked / jnp.sum(picked, axis=1, keepdims=True)
    flat_ids = routes.reshape(-1)
    expert_iota = jnp.arange(n_expert, dtype=jnp.int32)
    onehot = (flat_ids[:, None] == expert_iota[None, :]).astype(jnp.int32)
    earlier = jnp.cumsum(onehot, axis=0) - onehot
    slot_index = jnp.sum(earlier * onehot, axis=1)
    target = flat_ids * capacity + slot_index
    slot_iota = jnp.arange(n_expert * capacity, dtype=jnp.int32)
    placing = (slot_iota[:, None] == target[None, :]).astype(jnp.bfloat16)
    repeated = jnp.repeat(normed, 2, axis=0)
    send_slots = jnp.dot(placing, repeated, preferred_element_type=jnp.float32).astype(jnp.bfloat16)
    send_slots = send_slots.reshape(n_expert, capacity, width)
    received = lax.all_to_all(send_slots, "expert", split_axis=0, concat_axis=0, tiled=True)
    weights = jnp.concatenate(pieces, axis=1)
    gate_rows, up_rows, down_rows = weights[0], weights[1], weights[2]
    slot_total = n_expert * capacity
    rows_in = received.reshape(slot_total, width)
    peer_rows = [lax.ppermute(rows_in, "tx", shift_pairs(n_tx, s)) for s in range(1, n_tx)]
    own = expert_block(rows_in, gate_rows, up_rows, down_rows).astype(jnp.bfloat16)
    peer_rows = jnp.concatenate(peer_rows, axis=0)
    partial = expert_block(peer_rows, gate_rows, up_rows, down_rows).astype(jnp.bfloat16)
    partial = partial.reshape(n_tx - 1, slot_total, width)
    expert_sum = own.astype(jnp.float32)
    for s in range(1, n_tx):
        back = lax.ppermute(partial[s - 1], "tx", shift_pairs(n_tx, -s))
        expert_sum = expert_sum + back.astype(jnp.float32)
    expert_sum = expert_sum.astype(jnp.bfloat16)
    expert_out = expert_sum.reshape(n_expert, capacity, width)
    returned = lax.all_to_all(expert_out, "expert", split_axis=0, concat_axis=0, tiled=True)
    returned = returned.reshape(slot_total, width)
    per_route = lax.dot_general(
        placing, returned, (((0,), (0,)), ((), ())), preferred_element_type=jnp.float32
    )
    per_route = per_route.reshape(row_count, 2, width)
    mixed = jnp.sum(gate_weights[:, :, None] * per_route, axis=1)
    residual_out = (hidden_one.astype(jnp.float32) + mixed).astype(jnp.bfloat16)
    next_normed = rms_scale(residual_out, gain_second)
    return (residual_out, next_normed)


def shift_pairs(n, shift):
    return [(i, (i + shift) % n) for i in range(n)]


def split_tensor(n):
    inner = int(math.isqrt(n))
    while n % inner:
        inner -= 1
    return n // inner, inner


def solution(mesh):
    n_expert = mesh.shape["expert"]
    n_ty, n_tx = split_tensor(mesh.shape["tensor"])
    grid = Mesh(mesh.devices.reshape(n_expert, n_ty, n_tx), ROWS_AXES)
    rows = P(ROWS_AXES, None)
    placed = (
        rows,
        P(TENSOR_AXES, "expert"),
        P(TENSOR_AXES, None),
        P(),
        P(),
        rows,
        P("expert", TENSOR_AXES, None),
        P("expert", TENSOR_AXES, None),
        P("expert", TENSOR_AXES, None),
        P(),
    )
    return jax.shard_map(
        per_device,
        mesh=grid,
        in_specs=placed,
        out_specs=(rows, rows),
        check_vma=False,
    )
```

```python
import math

import jax
import jax.numpy as jnp
from jax import lax
from jax.sharding import Mesh
from jax.sharding import PartitionSpec as P

ROWS_AXES = ("expert", "ty", "tx")
TENSOR_AXES = ("ty", "tx")


def rms_scale(values, gain):
    wide = values.astype(jnp.float32)
    scale = lax.rsqrt(jnp.mean(wide * wide, axis=-1, keepdims=True) + 1e-06)
    return (wide * scale * gain).astype(jnp.bfloat16)


def expert_block(inputs, gate_rows, up_rows, down_rows):
    gate_part = lax.dot_general(
        inputs, gate_rows, (((1,), (1,)), ((), ())), preferred_element_type=jnp.float32
    )
    up_part = lax.dot_general(
        inputs, up_rows, (((1,), (1,)), ((), ())), preferred_element_type=jnp.float32
    )
    hid = (jax.nn.gelu(gate_part, approximate=True) * up_part).astype(jnp.bfloat16)
    return jnp.dot(hid, down_rows, preferred_element_type=jnp.float32)


def per_device(
    residual_in,
    attn_heads,
    out_proj,
    gain_first,
    router_weight,
    routes,
    w_gate,
    w_upward,
    w_downward,
    gain_second,
):
    row_count = residual_in.shape[0]
    width = residual_in.shape[1]
    n_expert = lax.axis_size("expert")
    capacity = 4 * row_count // n_expert

    n_ty = lax.axis_size("ty")
    n_tx = lax.axis_size("tx")
    ty = lax.axis_index("ty")
    tx = lax.axis_index("tx")
    core = lax.axis_index("expert") % 2
    half = width // 2
    my_cols = lax.dynamic_slice_in_dim(out_proj, core * half, half, axis=1)
    near = [my_cols] + [lax.ppermute(my_cols, "ty", shift_pairs(n_ty, s)) for s in range(1, n_ty)]
    near = jnp.stack(near)
    my_half = [near] + [lax.ppermute(near, "tx", shift_pairs(n_tx, s)) for s in range(1, n_tx)]
    my_half = jnp.stack(my_half)
    other_half = lax.ppermute(my_half, "expert", [(i, i ^ 1) for i in range(n_expert)])
    own_heads = lax.all_to_all(attn_heads, TENSOR_AXES, 1, 0, tiled=True)
    own_heads = own_heads.reshape(n_ty, n_tx, -1, row_count)
    from_y = (ty - jnp.arange(n_ty)) % n_ty
    from_x = (tx - jnp.arange(n_tx)) % n_tx
    own_heads = jnp.take(jnp.take(own_heads, from_y, axis=0), from_x, axis=1).swapaxes(0, 1)
    contract = (((0, 1, 2), (0, 1, 2)), ((), ()))
    proj_mine = lax.dot_general(own_heads, my_half, contract, preferred_element_type=jnp.float32)
    proj_other = lax.dot_general(own_heads, other_half, contract, preferred_element_type=jnp.float32)
    projected = jnp.where(
        core == 0,
        jnp.concatenate([proj_mine, proj_other], axis=1),
        jnp.concatenate([proj_other, proj_mine], axis=1),
    )

    stacked = jnp.concatenate([w_gate, w_upward, w_downward], axis=0)
    gathered = lax.all_gather(stacked, "ty", axis=1, tiled=True)

    hidden_one = (residual_in.astype(jnp.float32) + projected).astype(jnp.bfloat16)
    normed = rms_scale(hidden_one, gain_first)
    logits = jnp.dot(normed.astype(jnp.float32), router_weight, precision=lax.Precision.HIGHEST)
    router_probs = jax.nn.softmax(logits, axis=-1)
    picked = jnp.take_along_axis(router_probs, routes, axis=1)
    gate_weights = picked / jnp.sum(picked, axis=1, keepdims=True)
    flat_ids = routes.reshape(-1)
    expert_iota = jnp.arange(n_expert, dtype=jnp.int32)
    onehot = (flat_ids[:, None] == expert_iota[None, :]).astype(jnp.int32)
    earlier = jnp.cumsum(onehot, axis=0) - onehot
    slot_index = jnp.sum(earlier * onehot, axis=1)
    target = flat_ids * capacity + slot_index
    slot_iota = jnp.arange(n_expert * capacity, dtype=jnp.int32)
    placing = (slot_iota[:, None] == target[None, :]).astype(jnp.bfloat16)
    repeated = jnp.repeat(normed, 2, axis=0)
    send_slots = jnp.dot(placing, repeated, preferred_element_type=jnp.float32).astype(jnp.bfloat16)
    send_slots = send_slots.reshape(n_expert, capacity, width)
    received = lax.all_to_all(send_slots, "expert", split_axis=0, concat_axis=0, tiled=True)
    gate_rows, up_rows, down_rows = gathered[0], gathered[1], gathered[2]
    slot_total = n_expert * capacity
    rows_in = received.reshape(slot_total, width)
    peer_rows = [lax.ppermute(rows_in, "tx", shift_pairs(n_tx, s)) for s in range(1, n_tx)]
    own = expert_block(rows_in, gate_rows, up_rows, down_rows).astype(jnp.bfloat16)
    peer_rows = jnp.concatenate(peer_rows, axis=0)
    partial = expert_block(peer_rows, gate_rows, up_rows, down_rows).astype(jnp.bfloat16)
    partial = partial.reshape(n_tx - 1, slot_total, width)
    expert_sum = own.astype(jnp.float32)
    for s in range(1, n_tx):
        back = lax.ppermute(partial[s - 1], "tx", shift_pairs(n_tx, -s))
        expert_sum = expert_sum + back.astype(jnp.float32)
    expert_sum = expert_sum.astype(jnp.bfloat16)
    expert_out = expert_sum.reshape(n_expert, capacity, width)
    returned = lax.all_to_all(expert_out, "expert", split_axis=0, concat_axis=0, tiled=True)
    returned = returned.reshape(slot_total, width)
    per_route = lax.dot_general(
        placing, returned, (((0,), (0,)), ((), ())), preferred_element_type=jnp.float32
    )
    per_route = per_route.reshape(row_count, 2, width)
    mixed = jnp.sum(gate_weights[:, :, None] * per_route, axis=1)
    residual_out = (hidden_one.astype(jnp.float32) + mixed).astype(jnp.bfloat16)
    next_normed = rms_scale(residual_out, gain_second)
    return (residual_out, next_normed)


def shift_pairs(n, shift):
    return [(i, (i + shift) % n) for i in range(n)]


def split_tensor(n):
    inner = int(math.isqrt(n))
    while n % inner:
        inner -= 1
    return n // inner, inner


def solution(mesh):
    n_expert = mesh.shape["expert"]
    n_ty, n_tx = split_tensor(mesh.shape["tensor"])
    grid = Mesh(mesh.devices.reshape(n_expert, n_ty, n_tx), ROWS_AXES)
    rows = P(ROWS_AXES, None)
    placed = (
        rows,
        P(TENSOR_AXES, "expert"),
        P(TENSOR_AXES, None),
        P(),
        P(),
        rows,
        P("expert", TENSOR_AXES, None),
        P("expert", TENSOR_AXES, None),
        P("expert", TENSOR_AXES, None),
        P(),
    )
    return jax.shard_map(
        per_device,
        mesh=grid,
        in_specs=placed,
        out_specs=(rows, rows),
        check_vma=False,
    )
```

```python
import math

import jax
import jax.numpy as jnp
from jax import lax
from jax.sharding import Mesh
from jax.sharding import PartitionSpec as P

ROWS_AXES = ("expert", "ty", "tx")
TENSOR_AXES = ("ty", "tx")


def rms_scale(values, gain):
    wide = values.astype(jnp.float32)
    scale = lax.rsqrt(jnp.mean(wide * wide, axis=-1, keepdims=True) + 1e-06)
    return (wide * scale * gain).astype(jnp.bfloat16)


def expert_block(inputs, gate_rows, up_rows, down_rows):
    gate_part = lax.dot_general(
        inputs, gate_rows, (((1,), (1,)), ((), ())), preferred_element_type=jnp.float32
    )
    up_part = lax.dot_general(
        inputs, up_rows, (((1,), (1,)), ((), ())), preferred_element_type=jnp.float32
    )
    hid = (jax.nn.gelu(gate_part, approximate=True) * up_part).astype(jnp.bfloat16)
    return jnp.dot(hid, down_rows, preferred_element_type=jnp.float32)


def per_device(
    residual_in,
    attn_heads,
    out_proj,
    gain_first,
    router_weight,
    routes,
    w_gate,
    w_upward,
    w_downward,
    gain_second,
):
    row_count = residual_in.shape[0]
    width = residual_in.shape[1]
    n_expert = lax.axis_size("expert")
    capacity = 4 * row_count // n_expert

    n_ty = lax.axis_size("ty")
    n_tx = lax.axis_size("tx")
    ty = lax.axis_index("ty")
    tx = lax.axis_index("tx")
    core = lax.axis_index("expert") % 2
    half = width // 2
    my_cols = lax.dynamic_slice_in_dim(out_proj, core * half, half, axis=1)
    near = [my_cols] + [lax.ppermute(my_cols, "tx", shift_pairs(n_tx, s)) for s in range(1, n_tx)]
    near = jnp.stack(near)
    my_half = [near] + [lax.ppermute(near, "ty", shift_pairs(n_ty, s)) for s in range(1, n_ty)]
    my_half = jnp.stack(my_half)
    other_half = lax.ppermute(my_half, "expert", [(i, i ^ 1) for i in range(n_expert)])
    own_heads = lax.all_to_all(attn_heads, TENSOR_AXES, 1, 0, tiled=True)
    own_heads = own_heads.reshape(n_ty, n_tx, -1, row_count)
    from_y = (ty - jnp.arange(n_ty)) % n_ty
    from_x = (tx - jnp.arange(n_tx)) % n_tx
    own_heads = jnp.take(jnp.take(own_heads, from_y, axis=0), from_x, axis=1)
    contract = (((0, 1, 2), (0, 1, 2)), ((), ()))
    proj_mine = lax.dot_general(own_heads, my_half, contract, preferred_element_type=jnp.float32)
    proj_other = lax.dot_general(own_heads, other_half, contract, preferred_element_type=jnp.float32)
    projected = jnp.where(
        core == 0,
        jnp.concatenate([proj_mine, proj_other], axis=1),
        jnp.concatenate([proj_other, proj_mine], axis=1),
    )

    stacked = jnp.concatenate([w_gate, w_upward, w_downward], axis=0)
    if n_ty == 4:
        from_below = lax.ppermute(stacked, "ty", shift_pairs(n_ty, 1))
        from_above = lax.ppermute(stacked, "ty", shift_pairs(n_ty, -1))
        cut = stacked.shape[1] // 2
        far = jnp.concatenate(
            [
                lax.ppermute(from_below[:, :cut], "ty", shift_pairs(n_ty, 1)),
                lax.ppermute(from_above[:, cut:], "ty", shift_pairs(n_ty, -1)),
            ],
            axis=1,
        )
        pieces = [stacked, from_below, far, from_above]
    else:
        pieces = [stacked] + [
            lax.ppermute(stacked, "ty", shift_pairs(n_ty, s)) for s in range(1, n_ty)
        ]

    hidden_one = (residual_in.astype(jnp.float32) + projected).astype(jnp.bfloat16)
    normed = rms_scale(hidden_one, gain_first)
    logits = jnp.dot(normed.astype(jnp.float32), router_weight, precision=lax.Precision.HIGHEST)
    router_probs = jax.nn.softmax(logits, axis=-1)
    picked = jnp.take_along_axis(router_probs, routes, axis=1)
    gate_weights = picked / jnp.sum(picked, axis=1, keepdims=True)
    flat_ids = routes.reshape(-1)
    expert_iota = jnp.arange(n_expert, dtype=jnp.int32)
    onehot = (flat_ids[:, None] == expert_iota[None, :]).astype(jnp.int32)
    earlier = jnp.cumsum(onehot, axis=0) - onehot
    slot_index = jnp.sum(earlier * onehot, axis=1)
    target = flat_ids * capacity + slot_index
    slot_iota = jnp.arange(n_expert * capacity, dtype=jnp.int32)
    placing = (slot_iota[:, None] == target[None, :]).astype(jnp.bfloat16)
    repeated = jnp.repeat(normed, 2, axis=0)
    send_slots = jnp.dot(placing, repeated, preferred_element_type=jnp.float32).astype(jnp.bfloat16)
    send_slots = send_slots.reshape(n_expert, capacity, width)
    received = lax.all_to_all(send_slots, "expert", split_axis=0, concat_axis=0, tiled=True)
    weights = jnp.concatenate(pieces, axis=1)
    gate_rows, up_rows, down_rows = weights[0], weights[1], weights[2]
    slot_total = n_expert * capacity
    rows_in = received.reshape(slot_total, width)
    peer_rows = [lax.ppermute(rows_in, "tx", shift_pairs(n_tx, s)) for s in range(1, n_tx)]
    own = expert_block(rows_in, gate_rows, up_rows, down_rows).astype(jnp.bfloat16)
    peer_rows = jnp.concatenate(peer_rows, axis=0)
    partial = expert_block(peer_rows, gate_rows, up_rows, down_rows).astype(jnp.bfloat16)
    partial = partial.reshape(n_tx - 1, slot_total, width)
    expert_sum = own.astype(jnp.float32)
    for s in range(1, n_tx):
        back = lax.ppermute(partial[s - 1], "tx", shift_pairs(n_tx, -s))
        expert_sum = expert_sum + back.astype(jnp.float32)
    expert_sum = expert_sum.astype(jnp.bfloat16)
    expert_out = expert_sum.reshape(n_expert, capacity, width)
    returned = lax.all_to_all(expert_out, "expert", split_axis=0, concat_axis=0, tiled=True)
    returned = returned.reshape(slot_total, width)
    per_route = lax.dot_general(
        placing, returned, (((0,), (0,)), ((), ())), preferred_element_type=jnp.float32
    )
    per_route = per_route.reshape(row_count, 2, width)
    mixed = jnp.sum(gate_weights[:, :, None] * per_route, axis=1)
    residual_out = (hidden_one.astype(jnp.float32) + mixed).astype(jnp.bfloat16)
    next_normed = rms_scale(residual_out, gain_second)
    return (residual_out, next_normed)


def shift_pairs(n, shift):
    return [(i, (i + shift) % n) for i in range(n)]


def split_tensor(n):
    inner = int(math.isqrt(n))
    while n % inner:
        inner -= 1
    return n // inner, inner


def solution(mesh):
    n_expert = mesh.shape["expert"]
    n_ty, n_tx = split_tensor(mesh.shape["tensor"])
    grid = Mesh(mesh.devices.reshape(n_expert, n_ty, n_tx), ROWS_AXES)
    rows = P(ROWS_AXES, None)
    placed = (
        rows,
        P(TENSOR_AXES, "expert"),
        P(TENSOR_AXES, None),
        P(),
        P(),
        rows,
        P("expert", TENSOR_AXES, None),
        P("expert", TENSOR_AXES, None),
        P("expert", TENSOR_AXES, None),
        P(),
    )
    return jax.shard_map(
        per_device,
        mesh=grid,
        in_specs=placed,
        out_specs=(rows, rows),
        check_vma=False,
    )
```

```python
import math

import jax
import jax.numpy as jnp
from jax import lax
from jax.sharding import Mesh
from jax.sharding import PartitionSpec as P

ROWS_AXES = ("expert", "ty", "tx")
TENSOR_AXES = ("ty", "tx")


def rms_scale(values, gain):
    wide = values.astype(jnp.float32)
    scale = lax.rsqrt(jnp.mean(wide * wide, axis=-1, keepdims=True) + 1e-06)
    return (wide * scale * gain).astype(jnp.bfloat16)


def expert_block(inputs, gate_rows, up_rows, down_rows):
    gate_part = lax.dot_general(
        inputs, gate_rows, (((1,), (1,)), ((), ())), preferred_element_type=jnp.float32
    )
    up_part = lax.dot_general(
        inputs, up_rows, (((1,), (1,)), ((), ())), preferred_element_type=jnp.float32
    )
    hid = (jax.nn.gelu(gate_part, approximate=True) * up_part).astype(jnp.bfloat16)
    return jnp.dot(hid, down_rows, preferred_element_type=jnp.float32)


def per_device(
    residual_in,
    attn_heads,
    out_proj,
    gain_first,
    router_weight,
    routes,
    w_gate,
    w_upward,
    w_downward,
    gain_second,
):
    row_count = residual_in.shape[0]
    width = residual_in.shape[1]
    n_expert = lax.axis_size("expert")
    capacity = 4 * row_count // n_expert

    n_ty = lax.axis_size("ty")
    n_tx = lax.axis_size("tx")
    ty = lax.axis_index("ty")
    tx = lax.axis_index("tx")
    core = lax.axis_index("expert") % 2
    half = width // 2
    my_cols = lax.dynamic_slice_in_dim(out_proj, core * half, half, axis=1)
    near = [my_cols] + [lax.ppermute(my_cols, "tx", shift_pairs(n_tx, s)) for s in range(1, n_tx)]
    near = jnp.stack(near)
    my_half = [near] + [lax.ppermute(near, "ty", shift_pairs(n_ty, s)) for s in range(1, n_ty)]
    my_half = jnp.stack(my_half)
    other_half = lax.ppermute(my_half, "expert", [(i, i ^ 1) for i in range(n_expert)])
    own_heads = lax.all_to_all(attn_heads, TENSOR_AXES, 1, 0, tiled=True)
    own_heads = own_heads.reshape(n_ty, n_tx, -1, row_count)
    from_y = (ty - jnp.arange(n_ty)) % n_ty
    from_x = (tx - jnp.arange(n_tx)) % n_tx
    own_heads = jnp.take(jnp.take(own_heads, from_y, axis=0), from_x, axis=1)
    contract = (((0, 1, 2), (0, 1, 2)), ((), ()))
    proj_mine = lax.dot_general(own_heads, my_half, contract, preferred_element_type=jnp.float32)
    proj_other = lax.dot_general(own_heads, other_half, contract, preferred_element_type=jnp.float32)
    projected = jnp.where(
        core == 0,
        jnp.concatenate([proj_mine, proj_other], axis=1),
        jnp.concatenate([proj_other, proj_mine], axis=1),
    )

    stacked = jnp.concatenate([w_gate, w_upward, w_downward], axis=0)
    pieces = [stacked] + [
        lax.ppermute(stacked, "ty", shift_pairs(n_ty, s)) for s in range(1, n_ty)
    ]

    hidden_one = (residual_in.astype(jnp.float32) + projected).astype(jnp.bfloat16)
    normed = rms_scale(hidden_one, gain_first)
    logits = jnp.dot(normed.astype(jnp.float32), router_weight, precision=lax.Precision.HIGHEST)
    router_probs = jax.nn.softmax(logits, axis=-1)
    picked = jnp.take_along_axis(router_probs, routes, axis=1)
    gate_weights = picked / jnp.sum(picked, axis=1, keepdims=True)
    flat_ids = routes.reshape(-1)
    expert_iota = jnp.arange(n_expert, dtype=jnp.int32)
    onehot = (flat_ids[:, None] == expert_iota[None, :]).astype(jnp.int32)
    earlier = jnp.cumsum(onehot, axis=0) - onehot
    slot_index = jnp.sum(earlier * onehot, axis=1)
    target = flat_ids * capacity + slot_index
    slot_iota = jnp.arange(n_expert * capacity, dtype=jnp.int32)
    placing = (slot_iota[:, None] == target[None, :]).astype(jnp.bfloat16)
    repeated = jnp.repeat(normed, 2, axis=0)
    send_slots = jnp.dot(placing, repeated, preferred_element_type=jnp.float32).astype(jnp.bfloat16)
    send_slots = send_slots.reshape(n_expert, capacity, width)
    received = lax.all_to_all(send_slots, "expert", split_axis=0, concat_axis=0, tiled=True)
    weights = jnp.concatenate(pieces, axis=1)
    gate_rows, up_rows, down_rows = weights[0], weights[1], weights[2]
    slot_total = n_expert * capacity
    rows_in = received.reshape(slot_total, width)
    if n_tx == 4:
        from_below = lax.ppermute(rows_in, "tx", shift_pairs(n_tx, 1))
        from_above = lax.ppermute(rows_in, "tx", shift_pairs(n_tx, -1))
        cut = slot_total // 2
        far = jnp.concatenate(
            [
                lax.ppermute(from_below[:cut], "tx", shift_pairs(n_tx, 1)),
                lax.ppermute(from_above[cut:], "tx", shift_pairs(n_tx, -1)),
            ],
            axis=0,
        )
        peer_rows = [from_below, far, from_above]
    else:
        peer_rows = [lax.ppermute(rows_in, "tx", shift_pairs(n_tx, s)) for s in range(1, n_tx)]
    own = expert_block(rows_in, gate_rows, up_rows, down_rows).astype(jnp.bfloat16)
    peer_rows = jnp.concatenate(peer_rows, axis=0)
    partial = expert_block(peer_rows, gate_rows, up_rows, down_rows).astype(jnp.bfloat16)
    partial = partial.reshape(n_tx - 1, slot_total, width)
    expert_sum = own.astype(jnp.float32)
    for s in range(1, n_tx):
        back = lax.ppermute(partial[s - 1], "tx", shift_pairs(n_tx, -s))
        expert_sum = expert_sum + back.astype(jnp.float32)
    expert_sum = expert_sum.astype(jnp.bfloat16)
    expert_out = expert_sum.reshape(n_expert, capacity, width)
    returned = lax.all_to_all(expert_out, "expert", split_axis=0, concat_axis=0, tiled=True)
    returned = returned.reshape(slot_total, width)
    per_route = lax.dot_general(
        placing, returned, (((0,), (0,)), ((), ())), preferred_element_type=jnp.float32
    )
    per_route = per_route.reshape(row_count, 2, width)
    mixed = jnp.sum(gate_weights[:, :, None] * per_route, axis=1)
    residual_out = (hidden_one.astype(jnp.float32) + mixed).astype(jnp.bfloat16)
    next_normed = rms_scale(residual_out, gain_second)
    return (residual_out, next_normed)


def shift_pairs(n, shift):
    return [(i, (i + shift) % n) for i in range(n)]


def split_tensor(n):
    inner = int(math.isqrt(n))
    while n % inner:
        inner -= 1
    return n // inner, inner


def solution(mesh):
    n_expert = mesh.shape["expert"]
    n_ty, n_tx = split_tensor(mesh.shape["tensor"])
    grid = Mesh(mesh.devices.reshape(n_expert, n_ty, n_tx), ROWS_AXES)
    rows = P(ROWS_AXES, None)
    placed = (
        rows,
        P(TENSOR_AXES, "expert"),
        P(TENSOR_AXES, None),
        P(),
        P(),
        rows,
        P("expert", TENSOR_AXES, None),
        P("expert", TENSOR_AXES, None),
        P("expert", TENSOR_AXES, None),
        P(),
    )
    return jax.shard_map(
        per_device,
        mesh=grid,
        in_specs=placed,
        out_specs=(rows, rows),
        check_vma=False,
    )
```

```python
import math

import jax
import jax.numpy as jnp
from jax import lax
from jax.sharding import Mesh
from jax.sharding import PartitionSpec as P

ROWS_AXES = ("expert", "ty", "tx")
TENSOR_AXES = ("ty", "tx")


def rms_scale(values, gain):
    wide = values.astype(jnp.float32)
    scale = lax.rsqrt(jnp.mean(wide * wide, axis=-1, keepdims=True) + 1e-06)
    return (wide * scale * gain).astype(jnp.bfloat16)


def expert_block(inputs, gate_rows, up_rows, down_rows):
    gate_part = lax.dot_general(
        inputs, gate_rows, (((1,), (1,)), ((), ())), preferred_element_type=jnp.float32
    )
    up_part = lax.dot_general(
        inputs, up_rows, (((1,), (1,)), ((), ())), preferred_element_type=jnp.float32
    )
    hid = (jax.nn.gelu(gate_part, approximate=True) * up_part).astype(jnp.bfloat16)
    return jnp.dot(hid, down_rows, preferred_element_type=jnp.float32)


def per_device(
    residual_in,
    attn_heads,
    out_proj,
    gain_first,
    router_weight,
    routes,
    w_gate,
    w_upward,
    w_downward,
    gain_second,
):
    row_count = residual_in.shape[0]
    width = residual_in.shape[1]
    n_expert = lax.axis_size("expert")
    capacity = 4 * row_count // n_expert

    n_ty = lax.axis_size("ty")
    n_tx = lax.axis_size("tx")
    ty = lax.axis_index("ty")
    tx = lax.axis_index("tx")
    core = lax.axis_index("expert") % 2
    half = width // 2
    my_cols = lax.dynamic_slice_in_dim(out_proj, core * half, half, axis=1)
    near = [my_cols] + [lax.ppermute(my_cols, "tx", shift_pairs(n_tx, s)) for s in range(1, n_tx)]
    near = jnp.stack(near)
    my_half = [near] + [lax.ppermute(near, "ty", shift_pairs(n_ty, s)) for s in range(1, n_ty)]
    my_half = jnp.stack(my_half)
    other_half = lax.ppermute(my_half, "expert", [(i, i ^ 1) for i in range(n_expert)])
    own_heads = lax.all_to_all(attn_heads, TENSOR_AXES, 1, 0, tiled=True)
    own_heads = own_heads.reshape(n_ty, n_tx, -1, row_count)
    from_y = (ty - jnp.arange(n_ty)) % n_ty
    from_x = (tx - jnp.arange(n_tx)) % n_tx
    own_heads = jnp.take(jnp.take(own_heads, from_y, axis=0), from_x, axis=1)
    contract = (((0, 1, 2), (0, 1, 2)), ((), ()))
    proj_mine = lax.dot_general(own_heads, my_half, contract, preferred_element_type=jnp.float32)
    proj_other = lax.dot_general(own_heads, other_half, contract, preferred_element_type=jnp.float32)
    projected = jnp.where(
        core == 0,
        jnp.concatenate([proj_mine, proj_other], axis=1),
        jnp.concatenate([proj_other, proj_mine], axis=1),
    )

    stacked = jnp.concatenate([w_gate, w_upward, w_downward], axis=0)
    pieces = [stacked] + [
        lax.ppermute(stacked, "ty", shift_pairs(n_ty, s)) for s in range(1, n_ty)
    ]

    hidden_one = (residual_in.astype(jnp.float32) + projected).astype(jnp.bfloat16)
    normed = rms_scale(hidden_one, gain_first)
    logits = jnp.dot(normed.astype(jnp.float32), router_weight, precision=lax.Precision.HIGHEST)
    router_probs = jax.nn.softmax(logits, axis=-1)
    picked = jnp.take_along_axis(router_probs, routes, axis=1)
    gate_weights = picked / jnp.sum(picked, axis=1, keepdims=True)
    flat_ids = routes.reshape(-1)
    expert_iota = jnp.arange(n_expert, dtype=jnp.int32)
    onehot = (flat_ids[:, None] == expert_iota[None, :]).astype(jnp.int32)
    earlier = jnp.cumsum(onehot, axis=0) - onehot
    slot_index = jnp.sum(earlier * onehot, axis=1)
    target = flat_ids * capacity + slot_index
    slot_iota = jnp.arange(n_expert * capacity, dtype=jnp.int32)
    placing = (slot_iota[:, None] == target[None, :]).astype(jnp.bfloat16)
    repeated = jnp.repeat(normed, 2, axis=0)
    send_slots = jnp.dot(placing, repeated, preferred_element_type=jnp.float32).astype(jnp.bfloat16)
    send_slots = send_slots.reshape(n_expert, capacity, width)
    received = lax.all_to_all(send_slots, "expert", split_axis=0, concat_axis=0, tiled=True)
    weights = jnp.concatenate(pieces, axis=1)
    gate_rows, up_rows, down_rows = weights[0], weights[1], weights[2]
    slot_total = n_expert * capacity
    rows_in = received.reshape(slot_total, width)
    if n_tx == 4:
        from_below = lax.ppermute(rows_in, "tx", shift_pairs(n_tx, 1))
        from_above = lax.ppermute(rows_in, "tx", shift_pairs(n_tx, -1))
        cut = slot_total // 2
        far = jnp.concatenate(
            [
                lax.ppermute(from_below[:cut], "tx", shift_pairs(n_tx, 1)),
                lax.ppermute(from_above[cut:], "tx", shift_pairs(n_tx, -1)),
            ],
            axis=0,
        )
        peer_rows = [from_below, far, from_above]
    else:
        peer_rows = [lax.ppermute(rows_in, "tx", shift_pairs(n_tx, s)) for s in range(1, n_tx)]
    own = expert_block(rows_in, gate_rows, up_rows, down_rows).astype(jnp.bfloat16)
    peer_rows = jnp.concatenate(peer_rows, axis=0)
    partial = expert_block(peer_rows, gate_rows, up_rows, down_rows).astype(jnp.bfloat16)
    partial = partial.reshape(n_tx - 1, slot_total, width)
    expert_sum = own.astype(jnp.float32)
    if n_tx == 4:
        cut = slot_total // 2
        down_mail = jnp.concatenate([partial[0], partial[1][:cut]], axis=0)
        up_mail = jnp.concatenate([partial[2], partial[1][cut:]], axis=0)
        down_got = lax.ppermute(down_mail, "tx", shift_pairs(n_tx, -1))
        up_got = lax.ppermute(up_mail, "tx", shift_pairs(n_tx, 1))
        far_a = lax.ppermute(down_got[slot_total:], "tx", shift_pairs(n_tx, -1))
        far_b = lax.ppermute(up_got[slot_total:], "tx", shift_pairs(n_tx, 1))
        far = jnp.concatenate([far_a, far_b], axis=0)
        for back in (down_got[:slot_total], up_got[:slot_total], far):
            expert_sum = expert_sum + back.astype(jnp.float32)
    else:
        for s in range(1, n_tx):
            back = lax.ppermute(partial[s - 1], "tx", shift_pairs(n_tx, -s))
            expert_sum = expert_sum + back.astype(jnp.float32)
    expert_sum = expert_sum.astype(jnp.bfloat16)
    expert_out = expert_sum.reshape(n_expert, capacity, width)
    returned = lax.all_to_all(expert_out, "expert", split_axis=0, concat_axis=0, tiled=True)
    returned = returned.reshape(slot_total, width)
    per_route = lax.dot_general(
        placing, returned, (((0,), (0,)), ((), ())), preferred_element_type=jnp.float32
    )
    per_route = per_route.reshape(row_count, 2, width)
    mixed = jnp.sum(gate_weights[:, :, None] * per_route, axis=1)
    residual_out = (hidden_one.astype(jnp.float32) + mixed).astype(jnp.bfloat16)
    next_normed = rms_scale(residual_out, gain_second)
    return (residual_out, next_normed)


def shift_pairs(n, shift):
    return [(i, (i + shift) % n) for i in range(n)]


def split_tensor(n):
    inner = int(math.isqrt(n))
    while n % inner:
        inner -= 1
    return n // inner, inner


def solution(mesh):
    n_expert = mesh.shape["expert"]
    n_ty, n_tx = split_tensor(mesh.shape["tensor"])
    grid = Mesh(mesh.devices.reshape(n_expert, n_ty, n_tx), ROWS_AXES)
    rows = P(ROWS_AXES, None)
    placed = (
        rows,
        P(TENSOR_AXES, "expert"),
        P(TENSOR_AXES, None),
        P(),
        P(),
        rows,
        P("expert", TENSOR_AXES, None),
        P("expert", TENSOR_AXES, None),
        P("expert", TENSOR_AXES, None),
        P(),
    )
    return jax.shard_map(
        per_device,
        mesh=grid,
        in_specs=placed,
        out_specs=(rows, rows),
        check_vma=False,
    )
```

```python
import math

import jax
import jax.numpy as jnp
from jax import lax
from jax.sharding import Mesh
from jax.sharding import PartitionSpec as P

ROWS_AXES = ("expert", "ty", "tx")
TENSOR_AXES = ("ty", "tx")


def rms_scale(values, gain):
    wide = values.astype(jnp.float32)
    scale = lax.rsqrt(jnp.mean(wide * wide, axis=-1, keepdims=True) + 1e-06)
    return (wide * scale * gain).astype(jnp.bfloat16)


def expert_block(inputs, gate_rows, up_rows, down_rows):
    gate_part = lax.dot_general(
        inputs, gate_rows, (((1,), (1,)), ((), ())), preferred_element_type=jnp.float32
    )
    up_part = lax.dot_general(
        inputs, up_rows, (((1,), (1,)), ((), ())), preferred_element_type=jnp.float32
    )
    hid = (jax.nn.gelu(gate_part, approximate=True) * up_part).astype(jnp.bfloat16)
    return jnp.dot(hid, down_rows, preferred_element_type=jnp.float32)


def per_device(
    residual_in,
    attn_heads,
    out_proj,
    gain_first,
    router_weight,
    routes,
    w_gate,
    w_upward,
    w_downward,
    gain_second,
):
    row_count = residual_in.shape[0]
    width = residual_in.shape[1]
    n_expert = lax.axis_size("expert")
    capacity = 4 * row_count // n_expert

    n_ty = lax.axis_size("ty")
    n_tx = lax.axis_size("tx")
    ty = lax.axis_index("ty")
    tx = lax.axis_index("tx")
    core = lax.axis_index("expert") % 2
    half = width // 2
    my_cols = lax.dynamic_slice_in_dim(out_proj, core * half, half, axis=1)
    near = [my_cols] + [lax.ppermute(my_cols, "tx", shift_pairs(n_tx, s)) for s in range(1, n_tx)]
    near = jnp.stack(near)
    my_half = [near] + [lax.ppermute(near, "ty", shift_pairs(n_ty, s)) for s in range(1, n_ty)]
    my_half = jnp.stack(my_half)
    other_half = lax.ppermute(my_half, "expert", [(i, i ^ 1) for i in range(n_expert)])
    own_heads = lax.all_to_all(attn_heads, TENSOR_AXES, 1, 0, tiled=True)
    own_heads = own_heads.reshape(n_ty, n_tx, -1, row_count)
    from_y = (ty - jnp.arange(n_ty)) % n_ty
    from_x = (tx - jnp.arange(n_tx)) % n_tx
    own_heads = jnp.take(jnp.take(own_heads, from_y, axis=0), from_x, axis=1)
    contract = (((0, 1, 2), (0, 1, 2)), ((), ()))
    proj_mine = lax.dot_general(own_heads, my_half, contract, preferred_element_type=jnp.float32)
    proj_other = lax.dot_general(own_heads, other_half, contract, preferred_element_type=jnp.float32)
    projected = jnp.where(
        core == 0,
        jnp.concatenate([proj_mine, proj_other], axis=1),
        jnp.concatenate([proj_other, proj_mine], axis=1),
    )

    stacked = jnp.concatenate([w_gate, w_upward, w_downward], axis=0)
    pieces = [stacked] + [
        lax.ppermute(stacked, "ty", shift_pairs(n_ty, s)) for s in range(1, n_ty)
    ]

    hidden_one = (residual_in.astype(jnp.float32) + projected).astype(jnp.bfloat16)
    normed = rms_scale(hidden_one, gain_first)
    logits = jnp.dot(normed.astype(jnp.float32), router_weight, precision=lax.Precision.HIGHEST)
    router_probs = jax.nn.softmax(logits, axis=-1)
    picked = jnp.take_along_axis(router_probs, routes, axis=1)
    gate_weights = picked / jnp.sum(picked, axis=1, keepdims=True)
    flat_ids = routes.reshape(-1)
    expert_iota = jnp.arange(n_expert, dtype=jnp.int32)
    onehot = (flat_ids[:, None] == expert_iota[None, :]).astype(jnp.int32)
    earlier = jnp.cumsum(onehot, axis=0) - onehot
    slot_index = jnp.sum(earlier * onehot, axis=1)
    target = flat_ids * capacity + slot_index
    slot_iota = jnp.arange(n_expert * capacity, dtype=jnp.int32)
    placing = (slot_iota[:, None] == target[None, :]).astype(jnp.bfloat16)
    repeated = jnp.repeat(normed, 2, axis=0)
    send_slots = jnp.dot(placing, repeated, preferred_element_type=jnp.float32).astype(jnp.bfloat16)
    send_slots = send_slots.reshape(n_expert, capacity, width)
    received = lax.all_to_all(send_slots, "expert", split_axis=0, concat_axis=0, tiled=True)
    weights = jnp.concatenate(pieces, axis=1)
    gate_rows, up_rows, down_rows = weights[0], weights[1], weights[2]
    slot_total = n_expert * capacity
    rows_in = received.reshape(slot_total, width)
    if n_tx == 4:
        from_below = lax.ppermute(rows_in, "tx", shift_pairs(n_tx, 1))
        from_above = lax.ppermute(rows_in, "tx", shift_pairs(n_tx, -1))
        cut = slot_total // 2
        far = jnp.concatenate(
            [
                lax.ppermute(from_below[:cut], "tx", shift_pairs(n_tx, 1)),
                lax.ppermute(from_above[cut:], "tx", shift_pairs(n_tx, -1)),
            ],
            axis=0,
        )
        all_rows = [rows_in, from_below, far, from_above]
    else:
        all_rows = [rows_in] + [lax.ppermute(rows_in, "tx", shift_pairs(n_tx, s)) for s in range(1, n_tx)]
    all_rows = jnp.concatenate(all_rows, axis=0)
    partial = expert_block(all_rows, gate_rows, up_rows, down_rows).astype(jnp.bfloat16)
    partial = partial.reshape(n_tx, slot_total, width)
    expert_sum = partial[0].astype(jnp.float32)
    for s in range(1, n_tx):
        back = lax.ppermute(partial[s], "tx", shift_pairs(n_tx, -s))
        expert_sum = expert_sum + back.astype(jnp.float32)
    expert_sum = expert_sum.astype(jnp.bfloat16)
    expert_out = expert_sum.reshape(n_expert, capacity, width)
    returned = lax.all_to_all(expert_out, "expert", split_axis=0, concat_axis=0, tiled=True)
    returned = returned.reshape(slot_total, width)
    per_route = lax.dot_general(
        placing, returned, (((0,), (0,)), ((), ())), preferred_element_type=jnp.float32
    )
    per_route = per_route.reshape(row_count, 2, width)
    mixed = jnp.sum(gate_weights[:, :, None] * per_route, axis=1)
    residual_out = (hidden_one.astype(jnp.float32) + mixed).astype(jnp.bfloat16)
    next_normed = rms_scale(residual_out, gain_second)
    return (residual_out, next_normed)


def shift_pairs(n, shift):
    return [(i, (i + shift) % n) for i in range(n)]


def split_tensor(n):
    inner = int(math.isqrt(n))
    while n % inner:
        inner -= 1
    return n // inner, inner


def solution(mesh):
    n_expert = mesh.shape["expert"]
    n_ty, n_tx = split_tensor(mesh.shape["tensor"])
    grid = Mesh(mesh.devices.reshape(n_expert, n_ty, n_tx), ROWS_AXES)
    rows = P(ROWS_AXES, None)
    placed = (
        rows,
        P(TENSOR_AXES, "expert"),
        P(TENSOR_AXES, None),
        P(),
        P(),
        rows,
        P("expert", TENSOR_AXES, None),
        P("expert", TENSOR_AXES, None),
        P("expert", TENSOR_AXES, None),
        P(),
    )
    return jax.shard_map(
        per_device,
        mesh=grid,
        in_specs=placed,
        out_specs=(rows, rows),
        check_vma=False,
    )
```

```python
import math

import jax
import jax.numpy as jnp
from jax import lax
from jax.sharding import Mesh
from jax.sharding import PartitionSpec as P

ROWS_AXES = ("expert", "ty", "tx")
TENSOR_AXES = ("ty", "tx")


def rms_scale(values, gain):
    wide = values.astype(jnp.float32)
    scale = lax.rsqrt(jnp.mean(wide * wide, axis=-1, keepdims=True) + 1e-06)
    return (wide * scale * gain).astype(jnp.bfloat16)


def expert_block(inputs, gate_rows, up_rows, down_rows):
    gate_part = lax.dot_general(
        inputs, gate_rows, (((1,), (1,)), ((), ())), preferred_element_type=jnp.float32
    )
    up_part = lax.dot_general(
        inputs, up_rows, (((1,), (1,)), ((), ())), preferred_element_type=jnp.float32
    )
    hid = (jax.nn.gelu(gate_part, approximate=True) * up_part).astype(jnp.bfloat16)
    return jnp.dot(hid, down_rows, preferred_element_type=jnp.float32)


def per_device(
    residual_in,
    attn_heads,
    out_proj,
    gain_first,
    router_weight,
    routes,
    w_gate,
    w_upward,
    w_downward,
    gain_second,
):
    row_count = residual_in.shape[0]
    width = residual_in.shape[1]
    n_expert = lax.axis_size("expert")
    capacity = 4 * row_count // n_expert

    n_ty = lax.axis_size("ty")
    n_tx = lax.axis_size("tx")
    ty = lax.axis_index("ty")
    tx = lax.axis_index("tx")
    core = lax.axis_index("expert") % 2
    half = width // 2
    my_cols = lax.dynamic_slice_in_dim(out_proj, core * half, half, axis=1)
    near = [my_cols] + [lax.ppermute(my_cols, "tx", shift_pairs(n_tx, s)) for s in range(1, n_tx)]
    near = jnp.stack(near)
    my_half = [near] + [lax.ppermute(near, "ty", shift_pairs(n_ty, s)) for s in range(1, n_ty)]
    my_half = jnp.stack(my_half)
    other_half = lax.ppermute(my_half, "expert", [(i, i ^ 1) for i in range(n_expert)])
    own_heads = lax.all_to_all(attn_heads, TENSOR_AXES, 1, 0, tiled=True)
    own_heads = own_heads.reshape(n_ty, n_tx, -1, row_count)
    from_y = (ty - jnp.arange(n_ty)) % n_ty
    from_x = (tx - jnp.arange(n_tx)) % n_tx
    own_heads = jnp.take(jnp.take(own_heads, from_y, axis=0), from_x, axis=1)
    contract = (((0, 1, 2), (0, 1, 2)), ((), ()))
    proj_mine = lax.dot_general(own_heads, my_half, contract, preferred_element_type=jnp.float32)
    proj_other = lax.dot_general(own_heads, other_half, contract, preferred_element_type=jnp.float32)
    projected = jnp.where(
        core == 0,
        jnp.concatenate([proj_mine, proj_other], axis=1),
        jnp.concatenate([proj_other, proj_mine], axis=1),
    )

    stacked = jnp.concatenate([w_gate, w_upward, w_downward], axis=0)
    pieces = [stacked] + [
        lax.ppermute(stacked, "ty", shift_pairs(n_ty, s)) for s in range(1, n_ty)
    ]

    hidden_one = (residual_in.astype(jnp.float32) + projected).astype(jnp.bfloat16)
    normed = rms_scale(hidden_one, gain_first)
    logits = jnp.dot(normed.astype(jnp.float32), router_weight, precision=lax.Precision.HIGHEST)
    router_probs = jax.nn.softmax(logits, axis=-1)
    picked = jnp.take_along_axis(router_probs, routes, axis=1)
    gate_weights = picked / jnp.sum(picked, axis=1, keepdims=True)
    flat_ids = routes.reshape(-1)
    expert_iota = jnp.arange(n_expert, dtype=jnp.int32)
    onehot = (flat_ids[:, None] == expert_iota[None, :]).astype(jnp.int32)
    earlier = jnp.cumsum(onehot, axis=0) - onehot
    slot_index = jnp.sum(earlier * onehot, axis=1)
    target = flat_ids * capacity + slot_index
    slot_iota = jnp.arange(n_expert * capacity, dtype=jnp.int32).reshape(n_expert, capacity)
    placing = (slot_iota[:, :, None] == target[None, None, :]).astype(jnp.bfloat16)
    repeated = jnp.repeat(normed, 2, axis=0)
    send_slots = lax.dot_general(
        placing, repeated, (((2,), (0,)), ((), ())), preferred_element_type=jnp.float32
    ).astype(jnp.bfloat16)
    received = lax.all_to_all(send_slots, "expert", split_axis=0, concat_axis=0, tiled=True)
    weights = jnp.concatenate(pieces, axis=1)
    gate_rows, up_rows, down_rows = weights[0], weights[1], weights[2]
    slot_total = n_expert * capacity
    rows_in = received.reshape(slot_total, width)
    if n_tx == 4:
        from_below = lax.ppermute(rows_in, "tx", shift_pairs(n_tx, 1))
        from_above = lax.ppermute(rows_in, "tx", shift_pairs(n_tx, -1))
        cut = slot_total // 2
        far = jnp.concatenate(
            [
                lax.ppermute(from_below[:cut], "tx", shift_pairs(n_tx, 1)),
                lax.ppermute(from_above[cut:], "tx", shift_pairs(n_tx, -1)),
            ],
            axis=0,
        )
        peer_rows = [from_below, far, from_above]
    else:
        peer_rows = [lax.ppermute(rows_in, "tx", shift_pairs(n_tx, s)) for s in range(1, n_tx)]
    own = expert_block(rows_in, gate_rows, up_rows, down_rows).astype(jnp.bfloat16)
    peer_rows = jnp.concatenate(peer_rows, axis=0)
    partial = expert_block(peer_rows, gate_rows, up_rows, down_rows).astype(jnp.bfloat16)
    partial = partial.reshape(n_tx - 1, slot_total, width)
    expert_sum = own.astype(jnp.float32)
    for s in range(1, n_tx):
        back = lax.ppermute(partial[s - 1], "tx", shift_pairs(n_tx, -s))
        expert_sum = expert_sum + back.astype(jnp.float32)
    expert_sum = expert_sum.astype(jnp.bfloat16)
    expert_out = expert_sum.reshape(n_expert, capacity, width)
    returned = lax.all_to_all(expert_out, "expert", split_axis=0, concat_axis=0, tiled=True)
    per_route = lax.dot_general(
        placing, returned, (((0, 1), (0, 1)), ((), ())), preferred_element_type=jnp.float32
    )
    per_route = per_route.reshape(row_count, 2, width)
    mixed = jnp.sum(gate_weights[:, :, None] * per_route, axis=1)
    residual_out = (hidden_one.astype(jnp.float32) + mixed).astype(jnp.bfloat16)
    next_normed = rms_scale(residual_out, gain_second)
    return (residual_out, next_normed)


def shift_pairs(n, shift):
    return [(i, (i + shift) % n) for i in range(n)]


def split_tensor(n):
    inner = int(math.isqrt(n))
    while n % inner:
        inner -= 1
    return n // inner, inner


def solution(mesh):
    n_expert = mesh.shape["expert"]
    n_ty, n_tx = split_tensor(mesh.shape["tensor"])
    grid = Mesh(mesh.devices.reshape(n_expert, n_ty, n_tx), ROWS_AXES)
    rows = P(ROWS_AXES, None)
    placed = (
        rows,
        P(TENSOR_AXES, "expert"),
        P(TENSOR_AXES, None),
        P(),
        P(),
        rows,
        P("expert", TENSOR_AXES, None),
        P("expert", TENSOR_AXES, None),
        P("expert", TENSOR_AXES, None),
        P(),
    )
    return jax.shard_map(
        per_device,
        mesh=grid,
        in_specs=placed,
        out_specs=(rows, rows),
        check_vma=False,
    )
```
